256 devices in a mesh: dp: 8 (over x, core), seq: 32 (over z, y).
Axes of the slice: x: 4, y: 4, z: 8, core: 2. Of those that a mesh axis runs over, the one named last changes fastest.
Arguments:
- tokens: bfloat16 [32768, 2048], P(('dp', 'seq')), parts along dimension 0, may hold values from -6 to 6
- expert_ids: int32 [32768, 2], P(('dp', 'seq')), parts along dimension 0, may hold values from 0 to 31, all different within a row; in each aligned block of 128 rows (0 to 127, 128 to 255, ...) at most 16 rows name the same one
- router: bfloat16 [2048, 32], replicated, may hold values from -0.125 to 0.125
- w_gate: bfloat16 [32, 2048, 768], P('seq'), may hold values from -0.125 to 0.125
- w_up: bfloat16 [32, 2048, 768], P('seq'), may hold values from -0.125 to 0.125
- w_down: bfloat16 [32, 768, 2048], P('seq'), may hold values from -0.21875 to 0.21875
- spike_level: int32 [32, 768], P('seq'), may hold values from 1 to 8
- queries: bfloat16 [32768, 2048], P(('dp', 'seq')), parts along dimension 0, may hold values from -6 to 6
- key_vectors: bfloat16 [32768, 2048], P(('dp', 'seq')), parts along dimension 0, may hold values from -0.59765625 to 0.59765625
- log_decay: float32 [16, 32768], P(None, ('dp', 'seq')), parts along dimension 1, may hold values from -1 to 0
Outputs:
- expert_mix: bfloat16 [32768, 2048], P(('dp', 'seq')), parts along dimension 0
- attended: bfloat16 [32768, 2048], P(('dp', 'seq')), parts along dimension 0
The draws below stay inside these ranges and needn't reach their ends.
There are 8 independent parts, one for each index of `dp`. The reference program is written for one: setup_inputs(seed, part) draws one part's arguments, and reference() takes and returns one part's arrays. A program takes and returns all parts, laid end to end along the dimension named above; an argument that names none is the same for every part. Nothing has to cross between parts.
Inputs may be any that keep to these rules, and one draw needn't show every extreme that they name: `expert_ids`: each row names two different experts; among the rows of one device no expert is named more than 16 times.
All inputs are finite; a program needn't handle non-finite values.
Results may differ from the reference program's by a relative error of at most 0.0066.
Values may be sent and summed in bfloat16 or wider, within the bound.
No kernel may reach another device: no remote copies, remote signals or barrier semaphores. Data moves between devices by JAX's collectives and lax.ppermute only.
A program may use at most 128 MiB of HBM per device.

```python
import math
from functools import partial
import jax
import jax.numpy as jnp
import numpy as np
from jax import lax

D = 2048
FF = 768
QUERY_HEAD_SETS = 16
HEAD_DIM = 128
TOK_DEV = 128
EXPERTS = 32
CAP = 16
SEQUENCE_LENGTH = 4096


def draw_log_decay(key, part):
    random_subkeys = jax.random.split(key, 8)
    slow_share = 0.5
    slow_heads = jax.random.uniform(random_subkeys[0], (QUERY_HEAD_SETS,)) < slow_share
    slow_rate = jax.random.uniform(random_subkeys[1], (QUERY_HEAD_SETS,), minval=0.1, maxval=0.4) / SEQUENCE_LENGTH
    fast_rate = 2.3 / jax.random.uniform(random_subkeys[2], (QUERY_HEAD_SETS,), minval=30.0, maxval=50.0)
    head_rate = jnp.where(slow_heads, slow_rate, fast_rate)
    device_factor = jnp.repeat(jax.random.uniform(random_subkeys[3], (SEQUENCE_LENGTH // TOK_DEV,), minval=0.6, maxval=1.6), TOK_DEV)
    roughness = jax.random.uniform(random_subkeys[4], (QUERY_HEAD_SETS, SEQUENCE_LENGTH), minval=0.6, maxval=1.4)
    constant_portion = -head_rate[:, None] * device_factor[None, :] * roughness
    leading_spike = jax.random.randint(random_subkeys[5], (QUERY_HEAD_SETS,), 0, SEQUENCE_LENGTH)
    spike_shift = jax.random.randint(random_subkeys[7], (QUERY_HEAD_SETS,), 1, SEQUENCE_LENGTH)
    trailing_spike = (leading_spike + spike_shift) % SEQUENCE_LENGTH
    spike_locations = jnp.stack([leading_spike, trailing_spike], axis=1)
    spike_retained = jax.random.uniform(random_subkeys[6], (QUERY_HEAD_SETS, 2), minval=0.5, maxval=0.8)
    token_positions = jnp.arange(SEQUENCE_LENGTH)
    spike_matches = token_positions[None, None, :] == spike_locations[:, :, None]
    spike_portion = jnp.sum(jnp.where(spike_matches, jnp.log(spike_retained)[:, :, None], 0.0), axis=1)
    return (constant_portion + spike_portion).astype(jnp.float32)


def touch_ends(drawn, stream_key, low, high):
    dims = drawn.shape
    spot = [jax.random.randint(jax.random.fold_in(stream_key, axis), (), 0, dims[axis]) for axis in range(len(dims))]
    drawn = drawn.at[tuple(spot)].set(low)
    longest = dims.index(max(dims))
    spot[longest] = (spot[longest] + 1) % dims[longest]
    return drawn.at[tuple(spot)].set(high)


def steps_of(own_key, extent, cuts, low, high):
    level = 1.0
    for axis_at, parts in cuts:
        draws = jax.random.uniform(jax.random.fold_in(jax.random.fold_in(own_key, 6), axis_at), (parts,), jnp.float32, low / len(cuts), high / len(cuts))
        level = level * jnp.repeat(jnp.exp(draws), extent[axis_at] // parts).reshape((-1,) + (1,) * (len(extent) - 1 - axis_at))
    return level


def assign_block(own_key, own, number, rows, amount, top, limit, slope):
    order = jax.random.permutation(own_key, amount)
    heavy_load, common = load_shares(amount, rows * top, limit, slope, True), load_shares(amount, rows * top, limit, slope, False)
    places = jnp.arange(amount)

    def named(tallies, offset_by):
        used = int((tallies > 0).sum())
        fixed = max(1, used // 4)
        shifted = fixed + (places - fixed + offset_by * (used - fixed)) % max(1, amount - fixed)
        return jnp.zeros((amount,), jnp.int32).at[order[jnp.where(places < fixed, places, shifted)]].set(jnp.asarray(tallies, jnp.int32))

    tallies = jnp.where(number % 4 == 0, named(heavy_load, number // 4), named(common, number - number // 4 - 1))
    mixed = jax.random.permutation(jax.random.fold_in(own, 3), amount)
    giver, receiver = mixed[0:amount // 2 * 2:2], mixed[1:amount // 2 * 2:2]
    room = jnp.minimum(tallies[giver] - 1, limit - tallies[receiver]) // 2
    room = jnp.where((giver == order[0]) | (receiver == order[0]) | (tallies[receiver] == 0), 0, jnp.maximum(room, 0))
    shifted = jax.random.randint(jax.random.fold_in(own, 4), (amount // 2,), 0, 1 << 20) % (room + 1)
    tallies = tallies.at[giver].add(-shifted).at[receiver].add(shifted)
    members = jnp.searchsorted(jnp.cumsum(tallies), jnp.arange(rows * top), side="right").astype(jnp.int32)
    table = members.reshape(top, rows).T
    table = table[jax.random.permutation(jax.random.fold_in(own, 1), rows)]
    offset_by = jax.random.randint(jax.random.fold_in(own, 2), (rows, 1), 0, top)
    return jnp.take_along_axis(table, (jnp.arange(top)[None, :] + offset_by) % top, axis=1)


def load_shares(count, total, bound, skew, full):
    loads = [(1 << 20) // math.isqrt(standing ** skew) + 1 for standing in range(1, count + 1)]
    largest = bound if full else min(bound, max(-(-total // count), total * loads[0] // sum(loads)))
    least = 1 if total - largest >= count - 1 else 0
    holding, surplus = [largest] + [least] * (count - 1), total - largest - least * (count - 1)
    while surplus > 0:
        movable = [i for i in range(1, count) if holding[i] < largest] or [i for i in range(1, count) if holding[i] < bound]
        whole, budget = sum([loads[i] for i in movable]), surplus
        for i in movable:
            more = min(bound - holding[i], max(1, budget * loads[i] // whole), surplus)
            holding[i] = holding[i] + more
            surplus = surplus - more
    return np.array(holding)


def scatter_about(own_key, shape, scale, limit, cuts=(), kind=jnp.bfloat16):
    level = steps_of(own_key, shape, cuts, -0.22, 0.18) if cuts else 1.0
    drawn = jax.random.normal(own_key, shape, jnp.float32) * scale * level
    return jnp.minimum(jnp.maximum(drawn, -limit), limit).astype(kind)


def setup_inputs(seed: int = 0, part: int = 0) -> dict:
    splits = jax.random.split(jax.random.key(seed), 11)
    own_keys = jax.random.split(jax.random.fold_in(splits[10], part), 11)
    tokens = scatter_about(own_keys[0], (SEQUENCE_LENGTH, D), 1.0, 6.0, ((0, 32),))
    expert_ids_keys = jax.random.split(jax.random.fold_in(own_keys[1], 1), SEQUENCE_LENGTH // TOK_DEV)
    expert_ids_turns = jax.random.permutation(jax.random.fold_in(own_keys[1], 3), SEQUENCE_LENGTH // TOK_DEV)
    expert_ids = jax.vmap(lambda own, number: assign_block(jax.random.fold_in(own_keys[1], 2), own, number, TOK_DEV, EXPERTS, 2, CAP, 2))(expert_ids_keys, expert_ids_turns).reshape((SEQUENCE_LENGTH, 2))
    router = scatter_about(splits[2], (D, EXPERTS), D ** -0.5, 0.125)
    w_gate = scatter_about(splits[3], (EXPERTS, D, FF), D ** -0.5, 0.125, ((0, 32),))
    w_up = scatter_about(splits[4], (EXPERTS, D, FF), D ** -0.5, 0.125, ((0, 32),))
    w_down = scatter_about(splits[5], (EXPERTS, FF, D), FF ** -0.5, 0.21875, ((0, 32),))
    spike_level = touch_ends(jax.random.randint(splits[6], (EXPERTS, FF), 1, 9), jax.random.fold_in(splits[6], 1), 1, 8).astype(jnp.int32)
    queries = scatter_about(own_keys[7], (SEQUENCE_LENGTH, D), 1.0, 6.0, ((0, 32),))
    key_vectors = scatter_about(own_keys[8], (SEQUENCE_LENGTH, D), 0.1, 0.59765625, ((0, 32),))
    log_decay = draw_log_decay(jax.random.fold_in(jax.random.fold_in(splits[10], part), 71), part)
    return {"tokens": tokens, "expert_ids": expert_ids, "router": router, "w_gate": w_gate, "w_up": w_up, "w_down": w_down, "spike_level": spike_level, "queries": queries, "key_vectors": key_vectors, "log_decay": log_decay}


def slot_ranks(id_rows, expert_total):
    flat_ids = id_rows.reshape(-1)
    one_hot = (flat_ids[:, None] == jnp.arange(expert_total, dtype=jnp.int32)[None, :]).astype(jnp.int32)
    running = jnp.cumsum(one_hot, axis=0)
    return lax.optimization_barrier(jnp.sum(one_hot * running, axis=1)) - 1

def expert_apply(token_rows, gate_matrix, up_matrix, down_matrix, levels):
    gate_values = jnp.dot(token_rows, gate_matrix, preferred_element_type=jnp.float32)
    up_values = jnp.dot(token_rows, up_matrix, preferred_element_type=jnp.float32)
    hidden = jax.nn.silu(gate_values) * up_values
    threshold = 0.125 * levels.astype(jnp.float32)
    spikes = (threshold * jnp.tanh(hidden / threshold)).astype(jnp.bfloat16)
    return jnp.dot(spikes, down_matrix, preferred_element_type=jnp.float32).astype(jnp.bfloat16)

def attend_block(query_heads, key_heads, value_heads, decay_rows, carried):
    highest = lax.Precision.HIGHEST
    cumulative = jnp.cumsum(decay_rows, axis=1)
    length = decay_rows.shape[1]
    scores = jnp.einsum('thd,shd->hts', query_heads.astype(jnp.float32), key_heads.astype(jnp.float32), precision=highest)
    causal = jnp.arange(length)[:, None] >= jnp.arange(length)[None, :]
    spread = cumulative[:, :, None] - cumulative[:, None, :]
    decay = jnp.where(causal[None], jnp.exp(jnp.minimum(spread, 0.0)), 0.0)
    weights = (scores * decay).astype(jnp.bfloat16)
    intra = jnp.einsum('hts,shd->thd', weights.astype(jnp.float32), value_heads.astype(jnp.float32), precision=highest)
    inter = jnp.exp(cumulative).T[:, :, None] * jnp.einsum('thd,hde->the', query_heads.astype(jnp.float32), carried, precision=highest)
    total_out = intra + inter
    normed = total_out * lax.rsqrt(lax.optimization_barrier(jnp.mean(total_out * total_out, axis=2, keepdims=True)) + 1e-06)
    tail = jnp.exp(cumulative[:, -1:] - cumulative)
    local_state = jnp.einsum('shd,she->hde', key_heads.astype(jnp.float32) * tail.T[:, :, None], value_heads.astype(jnp.float32), precision=highest)
    return (normed.astype(jnp.bfloat16), local_state, jnp.exp(cumulative[:, -1]))

def reference(tokens, expert_ids, router, w_gate, w_up, w_down, spike_level, queries, key_vectors, log_decay):
    blocks = SEQUENCE_LENGTH // TOK_DEV
    logits = jnp.dot(tokens, router, preferred_element_type=jnp.float32)
    matches = (expert_ids[:, :, None] == jnp.arange(EXPERTS, dtype=jnp.int32)[None, None, :]).astype(jnp.float32)
    picked = lax.optimization_barrier(jnp.sum(logits[:, None, :] * matches, axis=2))
    gate_first = jax.nn.sigmoid(picked[:, 0] - picked[:, 1])
    gate_second = jax.nn.sigmoid(picked[:, 1] - picked[:, 0])
    id_blocks = expert_ids.reshape(blocks, TOK_DEV, 2)
    slots = jax.vmap(partial(slot_ranks, expert_total=EXPERTS))(id_blocks)
    flat_ids = id_blocks.reshape(blocks, 2 * TOK_DEV)
    position = (flat_ids * CAP + slots).astype(jnp.int32)
    entry_rows = (jnp.arange(blocks, dtype=jnp.int32)[:, None] * TOK_DEV + jnp.arange(2 * TOK_DEV, dtype=jnp.int32)[None, :] // 2 + 1).astype(jnp.int32)
    table = jnp.zeros((blocks, EXPERTS * CAP), jnp.int32).at[jnp.arange(blocks, dtype=jnp.int32)[:, None], position].set(entry_rows)
    table = table.reshape(blocks, EXPERTS, CAP).transpose(1, 0, 2).reshape(EXPERTS, blocks * CAP)
    padded = jnp.concatenate([jnp.zeros((1, D), tokens.dtype), tokens], axis=0)

    def one_expert(operands):
        rows_table, gate_matrix, up_matrix, down_matrix, levels = operands
        return expert_apply(padded[rows_table], gate_matrix, up_matrix, down_matrix, levels)
    outputs = lax.map(one_expert, (table, w_gate, w_up, w_down, spike_level)).reshape(EXPERTS, blocks, CAP, D)
    block_of = jnp.arange(SEQUENCE_LENGTH, dtype=jnp.int32) // TOK_DEV
    token_slots = slots.reshape(SEQUENCE_LENGTH, 2).astype(jnp.int32)
    first_out = outputs[expert_ids[:, 0], block_of, token_slots[:, 0]].astype(jnp.float32)
    second_out = outputs[expert_ids[:, 1], block_of, token_slots[:, 1]].astype(jnp.float32)
    expert_mix = (gate_first[:, None] * first_out + gate_second[:, None] * second_out).astype(jnp.bfloat16)
    query_heads = queries.reshape(blocks, TOK_DEV, QUERY_HEAD_SETS, HEAD_DIM)
    key_heads = key_vectors.reshape(blocks, TOK_DEV, QUERY_HEAD_SETS, HEAD_DIM)
    value_heads = expert_mix.reshape(blocks, TOK_DEV, QUERY_HEAD_SETS, HEAD_DIM)
    decay_blocks = log_decay.reshape(QUERY_HEAD_SETS, blocks, TOK_DEV).transpose(1, 0, 2)

    def block_step(carried, operands):
        query_block, key_block, value_block, decay_block = operands
        normed, local_state, total = attend_block(query_block, key_block, value_block, decay_block, carried)
        return (total[:, None, None] * carried + local_state, normed)
    start_state = jnp.zeros((QUERY_HEAD_SETS, HEAD_DIM, HEAD_DIM), jnp.float32)
    final_state, attended = lax.scan(block_step, start_state, (query_heads, key_heads, value_heads, decay_blocks))
    return (expert_mix, attended.reshape(SEQUENCE_LENGTH, D))
```

```python
import jax
import jax.numpy as jnp
from jax import lax
from jax.sharding import Mesh
from jax.sharding import PartitionSpec as P

SLOTS = 16
GROUP = 4


def expert_apply(token_rows, gate_matrix, up_matrix, down_matrix, levels):
    gate_values = jnp.dot(token_rows, gate_matrix, preferred_element_type=jnp.float32)
    up_values = jnp.dot(token_rows, up_matrix, preferred_element_type=jnp.float32)
    hidden = jax.nn.silu(gate_values) * up_values
    threshold = 0.125 * levels.astype(jnp.float32)
    spikes = (threshold * jnp.tanh(hidden / threshold)).astype(jnp.bfloat16)
    return jnp.dot(spikes, down_matrix, preferred_element_type=jnp.float32).astype(jnp.bfloat16)


def body(
    tokens, expert_ids, router, w_gate, w_up, w_down, spike_level, queries, key_vectors, log_decay
):
    highest = lax.Precision.HIGHEST
    seq_axes = ("sz", "sy")
    count, width = tokens.shape
    n_experts = router.shape[1]
    heads = log_decay.shape[0]
    hd = queries.shape[1] // heads
    n_sz = lax.axis_size("sz")
    n_sy = lax.axis_size("sy")
    zi = lax.axis_index("sz")
    yi = lax.axis_index("sy")
    quarter = heads // n_sy

    all_decay = lax.all_gather(log_decay, seq_axes, axis=0)
    group_keys = lax.all_gather(key_vectors, "sy", axis=0)

    logits = jnp.dot(tokens, router, preferred_element_type=jnp.float32)
    matches = (
        expert_ids[:, :, None] == jnp.arange(n_experts, dtype=jnp.int32)[None, None, :]
    ).astype(jnp.float32)
    picked = jnp.sum(logits[:, None, :] * matches, axis=2)
    gate_first = jax.nn.sigmoid(picked[:, 0] - picked[:, 1])
    gate_second = jax.nn.sigmoid(picked[:, 1] - picked[:, 0])

    flat_ids = expert_ids.reshape(-1)
    entries = flat_ids.shape[0]
    one_hot = (flat_ids[:, None] == jnp.arange(n_experts, dtype=jnp.int32)[None, :]).astype(
        jnp.bfloat16
    )
    lower = (
        jnp.arange(entries)[:, None] >= jnp.arange(entries)[None, :]
    ).astype(jnp.bfloat16)
    running = jnp.dot(lower, one_hot, preferred_element_type=jnp.float32)
    slots = (jnp.sum(running * one_hot.astype(jnp.float32), axis=1) - 1.0).astype(jnp.int32)
    dest = flat_ids * SLOTS + slots
    n_rows = n_experts * SLOTS
    select = (jnp.arange(n_rows, dtype=jnp.int32)[:, None] == dest[None, :]).astype(jnp.bfloat16)
    select_tok = select.reshape(n_rows, count, 2).sum(axis=2)
    send = jnp.dot(select_tok, tokens, preferred_element_type=jnp.float32).astype(jnp.bfloat16)

    recv = lax.all_to_all(send.reshape(n_experts, SLOTS, width), seq_axes, 0, 0, tiled=True)
    computed = expert_apply(
        recv.reshape(n_rows, width), w_gate[0], w_up[0], w_down[0], spike_level[0]
    )
    back = lax.all_to_all(computed.reshape(n_experts, SLOTS, width), seq_axes, 0, 0, tiled=True)
    back = back.reshape(n_rows, width)

    dest2 = dest.reshape(count, 2)
    pick0 = (dest2[:, 0:1] == jnp.arange(n_rows, dtype=jnp.int32)[None, :]).astype(jnp.bfloat16)
    pick1 = (dest2[:, 1:2] == jnp.arange(n_rows, dtype=jnp.int32)[None, :]).astype(jnp.bfloat16)
    first_out = jnp.dot(pick0, back, preferred_element_type=jnp.float32)
    second_out = jnp.dot(pick1, back, preferred_element_type=jnp.float32)
    expert_mix = (gate_first[:, None] * first_out + gate_second[:, None] * second_out).astype(
        jnp.bfloat16
    )

    query_heads = queries.reshape(count, heads, hd)
    key_heads = key_vectors.reshape(count, heads, hd)
    value_heads = expert_mix.reshape(count, heads, hd)
    cumulative = jnp.cumsum(log_decay, axis=1)
    scores = jnp.einsum("thd,shd->hts", query_heads, key_heads, preferred_element_type=jnp.float32)
    causal = jnp.arange(count)[:, None] >= jnp.arange(count)[None, :]
    spread = cumulative[:, :, None] - cumulative[:, None, :]
    decay = jnp.where(causal[None], jnp.exp(jnp.minimum(spread, 0.0)), 0.0)
    weights = (scores * decay).astype(jnp.bfloat16)
    intra = jnp.einsum("hts,shd->thd", weights, value_heads, preferred_element_type=jnp.float32)

    group_values = lax.all_gather(expert_mix, "sy", axis=0)
    all_cum = jnp.cumsum(all_decay, axis=2)
    all_total = jnp.exp(all_cum[:, :, -1])
    group_cum = lax.dynamic_slice_in_dim(all_cum, zi * n_sy, n_sy, axis=0)
    group_tail = jnp.exp(group_cum[:, :, -1:] - group_cum)
    gk = group_keys.reshape(n_sy, count, heads, hd).astype(jnp.float32)
    gk = gk * jnp.transpose(group_tail, (0, 2, 1))[:, :, :, None]
    gv = group_values.reshape(n_sy, count, heads, hd).astype(jnp.float32)
    local_states = jnp.einsum("gshd,gshe->ghde", gk, gv, precision=highest)
    group_total = lax.dynamic_slice_in_dim(all_total, zi * n_sy, n_sy, axis=0)

    run = jnp.zeros((heads, hd, hd), jnp.float32)
    prefixes = [run]
    for g in range(n_sy):
        run = group_total[g][:, None, None] * run + local_states[g]
        prefixes.append(run)
    prefixes = jnp.stack(prefixes)
    inside = lax.dynamic_index_in_dim(prefixes, yi, 0, False)
    group_state = prefixes[n_sy]

    piece = lax.dynamic_slice_in_dim(group_state, yi * quarter, quarter, axis=0)
    pieces = lax.all_gather(piece, "sz", axis=0)
    group_decay = jnp.prod(all_total.reshape(n_sz, n_sy, heads), axis=1)
    quarter_decay = lax.dynamic_slice_in_dim(group_decay, yi * quarter, quarter, axis=1)
    run = jnp.zeros((quarter, hd, hd), jnp.float32)
    entering = [run]
    for g in range(n_sz - 1):
        run = quarter_decay[g][:, None, None] * run + pieces[g]
        entering.append(run)
    entering = jnp.stack(entering)
    mine = lax.dynamic_index_in_dim(entering, zi, 0, False)
    carried_groups = lax.all_gather(mine, "sy", axis=0).reshape(heads, hd, hd)

    lead = [jnp.ones((heads,), jnp.float32)]
    for g in range(n_sy - 1):
        lead.append(lead[-1] * group_total[g])
    lead = lax.dynamic_index_in_dim(jnp.stack(lead), yi, 0, False)
    carried = lead[:, None, None] * carried_groups + inside

    inter = jnp.exp(cumulative).T[:, :, None] * jnp.einsum(
        "thd,hde->the", query_heads.astype(jnp.float32), carried, precision=highest
    )
    total_out = intra + inter
    normed = total_out * lax.rsqrt(jnp.mean(total_out * total_out, axis=2, keepdims=True) + 1e-06)
    attended = normed.astype(jnp.bfloat16).reshape(count, heads * hd)
    return (expert_mix, attended)


def solution(mesh):
    n_dp = mesh.shape["dp"]
    n_seq = mesh.shape["seq"]
    inner = Mesh(mesh.devices.reshape(n_dp, n_seq // GROUP, GROUP), ("dp", "sz", "sy"))
    rows = ("dp", "sz", "sy")
    in_specs = (
        P(rows, None),
        P(rows, None),
        P(),
        P(("sz", "sy"), None, None),
        P(("sz", "sy"), None, None),
        P(("sz", "sy"), None, None),
        P(("sz", "sy"), None),
        P(rows, None),
        P(rows, None),
        P(None, rows),
    )
    out_specs = (P(rows, None), P(rows, None))
    return jax.shard_map(body, mesh=inner, in_specs=in_specs, out_specs=out_specs, check_vma=False)
```

```python
import jax
import jax.numpy as jnp
from jax import lax
from jax.sharding import Mesh
from jax.sharding import PartitionSpec as P

SLOTS = 16
GROUP = 4


def expert_apply(token_rows, gate_matrix, up_matrix, down_matrix, levels):
    gate_values = jnp.dot(token_rows, gate_matrix, preferred_element_type=jnp.float32)
    up_values = jnp.dot(token_rows, up_matrix, preferred_element_type=jnp.float32)
    hidden = jax.nn.silu(gate_values) * up_values
    threshold = 0.125 * levels.astype(jnp.float32)
    spikes = (threshold * jnp.tanh(hidden / threshold)).astype(jnp.bfloat16)
    return jnp.dot(spikes, down_matrix, preferred_element_type=jnp.float32).astype(jnp.bfloat16)


def body(
    tokens, expert_ids, router, w_gate, w_up, w_down, spike_level, queries, key_vectors, log_decay
):
    highest = lax.Precision.HIGHEST
    seq_axes = ("sz", "sy")
    count, width = tokens.shape
    n_experts = router.shape[1]
    heads = log_decay.shape[0]
    hd = queries.shape[1] // heads
    n_sz = lax.axis_size("sz")
    n_sy = lax.axis_size("sy")
    zi = lax.axis_index("sz")
    yi = lax.axis_index("sy")
    quarter = heads // n_sy

    qw = quarter * hd
    flat_decay = log_decay.reshape(n_sy, 1, quarter * count)
    decay_hi = lax.reduce_precision(flat_decay, exponent_bits=8, mantissa_bits=7)
    rest = flat_decay - decay_hi
    decay_mid = lax.reduce_precision(rest, exponent_bits=8, mantissa_bits=7)
    decay_lo = rest - decay_mid
    decay_parts = jnp.concatenate([decay_hi, decay_mid, decay_lo], axis=1).astype(jnp.bfloat16)
    q_split = queries.reshape(count, n_sy, qw).transpose(1, 0, 2)
    k_split = key_vectors.reshape(count, n_sy, qw).transpose(1, 0, 2)
    pad_rows = (-(2 * count + 3)) % 16
    packed = jnp.concatenate(
        [q_split, k_split, decay_parts, jnp.zeros((n_sy, pad_rows, qw), jnp.bfloat16)], axis=1
    )
    got = lax.all_to_all(packed, "sy", 0, 0, tiled=True)
    group_q = got[:, :count].reshape(n_sy, count, quarter, hd)
    group_k = got[:, count : 2 * count].reshape(n_sy, count, quarter, hd)
    parts = got[:, 2 * count : 2 * count + 3].astype(jnp.float32)
    group_decay = (parts[:, 0] + parts[:, 1] + parts[:, 2]).reshape(n_sy, quarter, count)

    logits = jnp.dot(tokens, router, preferred_element_type=jnp.float32)
    matches = (
        expert_ids[:, :, None] == jnp.arange(n_experts, dtype=jnp.int32)[None, None, :]
    ).astype(jnp.float32)
    picked = jnp.sum(logits[:, None, :] * matches, axis=2)
    gate_first = jax.nn.sigmoid(picked[:, 0] - picked[:, 1])
    gate_second = jax.nn.sigmoid(picked[:, 1] - picked[:, 0])

    flat_ids = expert_ids.reshape(-1)
    entries = flat_ids.shape[0]
    one_hot = (flat_ids[:, None] == jnp.arange(n_experts, dtype=jnp.int32)[None, :]).astype(
        jnp.bfloat16
    )
    lower = (
        jnp.arange(entries)[:, None] >= jnp.arange(entries)[None, :]
    ).astype(jnp.bfloat16)
    running = jnp.dot(lower, one_hot, preferred_element_type=jnp.float32)
    slots = (jnp.sum(running * one_hot.astype(jnp.float32), axis=1) - 1.0).astype(jnp.int32)
    dest = flat_ids * SLOTS + slots
    n_rows = n_experts * SLOTS
    select = (jnp.arange(n_rows, dtype=jnp.int32)[:, None] == dest[None, :]).astype(jnp.bfloat16)
    select_tok = select.reshape(n_rows, count, 2).sum(axis=2)
    send = jnp.dot(select_tok, tokens, preferred_element_type=jnp.float32).astype(jnp.bfloat16)

    recv = lax.all_to_all(send.reshape(n_experts, SLOTS, width), seq_axes, 0, 0, tiled=True)
    computed = expert_apply(
        recv.reshape(n_rows, width), w_gate[0], w_up[0], w_down[0], spike_level[0]
    )
    back = lax.all_to_all(computed.reshape(n_experts, SLOTS, width), seq_axes, 0, 0, tiled=True)
    back = back.reshape(n_rows, width)

    dest2 = dest.reshape(count, 2)
    pick0 = (dest2[:, 0:1] == jnp.arange(n_rows, dtype=jnp.int32)[None, :]).astype(jnp.bfloat16)
    pick1 = (dest2[:, 1:2] == jnp.arange(n_rows, dtype=jnp.int32)[None, :]).astype(jnp.bfloat16)
    first_out = jnp.dot(pick0, back, preferred_element_type=jnp.float32)
    second_out = jnp.dot(pick1, back, preferred_element_type=jnp.float32)
    expert_mix = (gate_first[:, None] * first_out + gate_second[:, None] * second_out).astype(
        jnp.bfloat16
    )

    v_split = expert_mix.reshape(count, n_sy, qw).transpose(1, 0, 2)
    group_v = lax.all_to_all(v_split, "sy", 0, 0, tiled=True).reshape(n_sy, count, quarter, hd)
    cumulative = jnp.cumsum(group_decay, axis=2)
    scores = jnp.einsum(
        "bthd,bshd->bhts", group_q, group_k, preferred_element_type=jnp.float32
    )
    causal = jnp.arange(count)[:, None] >= jnp.arange(count)[None, :]
    spread = cumulative[:, :, :, None] - cumulative[:, :, None, :]
    decay = jnp.where(causal[None, None], jnp.exp(jnp.minimum(spread, 0.0)), 0.0)
    weights = (scores * decay).astype(jnp.bfloat16)
    intra = jnp.einsum("bhts,bshd->bthd", weights, group_v, preferred_element_type=jnp.float32)

    tail = jnp.exp(cumulative[:, :, -1:] - cumulative)
    scaled_k = group_k.astype(jnp.float32) * jnp.transpose(tail, (0, 2, 1))[:, :, :, None]
    local_states = jnp.einsum(
        "bshd,bshe->bhde", scaled_k, group_v.astype(jnp.float32), precision=highest
    )
    block_total = jnp.exp(cumulative[:, :, -1])

    run = jnp.zeros((quarter, hd, hd), jnp.float32)
    lead = jnp.ones((quarter,), jnp.float32)
    inside, leads = [], []
    for b in range(n_sy):
        inside.append(run)
        leads.append(lead)
        run = block_total[b][:, None, None] * run + local_states[b]
        lead = lead * block_total[b]
    group_state, group_span = run, lead

    decay_row = jnp.zeros((8, hd), jnp.float32).at[0, :quarter].set(group_span)
    piece_packed = jnp.concatenate([group_state.reshape(quarter * hd, hd), decay_row], axis=0)
    pieces_packed = lax.all_gather(piece_packed, "sz", axis=0)
    pieces = pieces_packed[:, : quarter * hd].reshape(n_sz, quarter, hd, hd)
    spans = pieces_packed[:, quarter * hd, :quarter]
    run = jnp.zeros((quarter, hd, hd), jnp.float32)
    entering = [run]
    for g in range(n_sz - 1):
        run = spans[g][:, None, None] * run + pieces[g]
        entering.append(run)
    before = lax.dynamic_index_in_dim(jnp.stack(entering), zi, 0, False)

    carried = jnp.stack(leads)[:, :, None, None] * before[None] + jnp.stack(inside)
    inter = jnp.transpose(jnp.exp(cumulative), (0, 2, 1))[:, :, :, None] * jnp.einsum(
        "bthd,bhde->bthe", group_q.astype(jnp.float32), carried, precision=highest
    )
    total_out = intra + inter
    normed = total_out * lax.rsqrt(jnp.mean(total_out * total_out, axis=3, keepdims=True) + 1e-06)
    pieces_out = normed.astype(jnp.bfloat16).reshape(n_sy, count, qw)
    mine = lax.all_to_all(pieces_out, "sy", 0, 0, tiled=True)
    attended = mine.transpose(1, 0, 2).reshape(count, heads * hd)
    return (expert_mix, attended)


def solution(mesh):
    n_dp = mesh.shape["dp"]
    n_seq = mesh.shape["seq"]
    inner = Mesh(mesh.devices.reshape(n_dp, n_seq // GROUP, GROUP), ("dp", "sz", "sy"))
    rows = ("dp", "sz", "sy")
    in_specs = (
        P(rows, None),
        P(rows, None),
        P(),
        P(("sz", "sy"), None, None),
        P(("sz", "sy"), None, None),
        P(("sz", "sy"), None, None),
        P(("sz", "sy"), None),
        P(rows, None),
        P(rows, None),
        P(None, rows),
    )
    out_specs = (P(rows, None), P(rows, None))
    return jax.shard_map(body, mesh=inner, in_specs=in_specs, out_specs=out_specs, check_vma=False)
```

```python
import jax
import jax.numpy as jnp
from jax import lax
from jax.sharding import Mesh
from jax.sharding import PartitionSpec as P

SLOTS = 16
GROUP = 4


def expert_apply(token_rows, gate_matrix, up_matrix, down_matrix, levels):
    gate_values = jnp.dot(token_rows, gate_matrix, preferred_element_type=jnp.float32)
    up_values = jnp.dot(token_rows, up_matrix, preferred_element_type=jnp.float32)
    hidden = jax.nn.silu(gate_values) * up_values
    threshold = 0.125 * levels.astype(jnp.float32)
    spikes = (threshold * jnp.tanh(hidden / threshold)).astype(jnp.bfloat16)
    return jnp.dot(spikes, down_matrix, preferred_element_type=jnp.float32).astype(jnp.bfloat16)


def split3(values):
    hi = lax.reduce_precision(values, exponent_bits=8, mantissa_bits=7)
    rest = values - hi
    mid = lax.reduce_precision(rest, exponent_bits=8, mantissa_bits=7)
    return [hi, mid, rest - mid]


def body(
    tokens, expert_ids, router, w_gate, w_up, w_down, spike_level, queries, key_vectors, log_decay
):
    highest = lax.Precision.HIGHEST
    seq_axes = ("sz", "sy")
    count, width = tokens.shape
    n_experts = router.shape[1]
    heads = log_decay.shape[0]
    hd = queries.shape[1] // heads
    n_sz = lax.axis_size("sz")
    n_sy = lax.axis_size("sy")
    zi = lax.axis_index("sz")
    quarter = heads // n_sy
    qw = quarter * hd

    logits = jnp.dot(tokens, router, preferred_element_type=jnp.float32)
    matches = (
        expert_ids[:, :, None] == jnp.arange(n_experts, dtype=jnp.int32)[None, None, :]
    ).astype(jnp.float32)
    picked = jnp.sum(logits[:, None, :] * matches, axis=2)
    gate_first = jax.nn.sigmoid(picked[:, 0] - picked[:, 1])
    gate_second = jax.nn.sigmoid(picked[:, 1] - picked[:, 0])

    flat_ids = expert_ids.reshape(-1)
    entries = flat_ids.shape[0]
    one_hot = (flat_ids[:, None] == jnp.arange(n_experts, dtype=jnp.int32)[None, :]).astype(
        jnp.bfloat16
    )
    lower = (
        jnp.arange(entries)[:, None] >= jnp.arange(entries)[None, :]
    ).astype(jnp.bfloat16)
    running = jnp.dot(lower, one_hot, preferred_element_type=jnp.float32)
    slots = (jnp.sum(running * one_hot.astype(jnp.float32), axis=1) - 1.0).astype(jnp.int32)
    dest = flat_ids * SLOTS + slots
    n_rows = n_experts * SLOTS
    select = (jnp.arange(n_rows, dtype=jnp.int32)[:, None] == dest[None, :]).astype(jnp.bfloat16)
    select_tok = select.reshape(n_rows, count, 2).sum(axis=2)
    send = jnp.dot(select_tok, tokens, preferred_element_type=jnp.float32).astype(jnp.bfloat16)

    decay_parts = jnp.concatenate(split3(log_decay.reshape(n_sy, 1, quarter * count)), axis=1)
    slot_pairs = slots.reshape(count, 2).astype(jnp.float32)
    id_pairs = expert_ids.astype(jnp.float32)
    fields = [id_pairs[:, 0], slot_pairs[:, 0], id_pairs[:, 1], slot_pairs[:, 1]]
    fields += split3(gate_first) + split3(gate_second)
    n_fields = len(fields)
    info_rows = -(-(n_fields * count) // qw)
    info = jnp.stack(fields).reshape(-1)
    info = jnp.pad(info, (0, info_rows * qw - n_fields * count)).reshape(1, info_rows, qw)
    info = jnp.broadcast_to(info, (n_sy, info_rows, qw))
    q_split = queries.reshape(count, n_sy, qw).transpose(1, 0, 2)
    k_split = key_vectors.reshape(count, n_sy, qw).transpose(1, 0, 2)
    used = 2 * count + 3 + info_rows
    packed = jnp.concatenate(
        [
            q_split,
            k_split,
            decay_parts.astype(jnp.bfloat16),
            info.astype(jnp.bfloat16),
            jnp.zeros((n_sy, (-used) % 16, qw), jnp.bfloat16),
        ],
        axis=1,
    )
    got = lax.all_to_all(packed, "sy", 0, 0, tiled=True)
    group_q = got[:, :count].reshape(n_sy, count, quarter, hd)
    group_k = got[:, count : 2 * count].reshape(n_sy, count, quarter, hd)
    parts = got[:, 2 * count : 2 * count + 3].astype(jnp.float32)
    group_decay = (parts[:, 0] + parts[:, 1] + parts[:, 2]).reshape(n_sy, quarter, count)
    got_info = got[:, 2 * count + 3 : used].astype(jnp.float32).reshape(n_sy, info_rows * qw)
    got_info = got_info[:, : n_fields * count].reshape(n_sy, n_fields, count)
    g_first = (got_info[:, 4] + got_info[:, 5]) + got_info[:, 6]
    g_second = (got_info[:, 7] + got_info[:, 8]) + got_info[:, 9]
    row_first = (got_info[:, 0] * SLOTS + got_info[:, 1]).astype(jnp.int32)
    row_second = (got_info[:, 2] * SLOTS + got_info[:, 3]).astype(jnp.int32)

    recv = lax.all_to_all(send.reshape(n_experts, SLOTS, width), seq_axes, 0, 0, tiled=True)
    computed = expert_apply(
        recv.reshape(n_rows, width), w_gate[0], w_up[0], w_down[0], spike_level[0]
    )
    outgoing = computed.reshape(n_sz, n_sy, SLOTS, n_sy, qw).transpose(0, 3, 1, 2, 4)
    back = lax.all_to_all(outgoing.reshape(n_sz * n_sy, -1), seq_axes, 0, 0, tiled=True)
    table = back.reshape(n_experts, n_sy, SLOTS, qw).transpose(1, 0, 2, 3)
    table = table.reshape(n_sy, n_rows, qw)
    lanes = jnp.arange(n_rows, dtype=jnp.int32)[None, None, :]
    pick0 = (row_first[:, :, None] == lanes).astype(jnp.bfloat16)
    pick1 = (row_second[:, :, None] == lanes).astype(jnp.bfloat16)
    first_out = jnp.einsum("btr,brc->btc", pick0, table, preferred_element_type=jnp.float32)
    second_out = jnp.einsum("btr,brc->btc", pick1, table, preferred_element_type=jnp.float32)
    mix_q = (g_first[:, :, None] * first_out + g_second[:, :, None] * second_out).astype(
        jnp.bfloat16
    )

    group_v = mix_q.reshape(n_sy, count, quarter, hd)
    cumulative = jnp.cumsum(group_decay, axis=2)
    scores = jnp.einsum(
        "bthd,bshd->bhts", group_q, group_k, preferred_element_type=jnp.float32
    )
    causal = jnp.arange(count)[:, None] >= jnp.arange(count)[None, :]
    spread = cumulative[:, :, :, None] - cumulative[:, :, None, :]
    decay = jnp.where(causal[None, None], jnp.exp(jnp.minimum(spread, 0.0)), 0.0)
    weights = (scores * decay).astype(jnp.bfloat16)
    intra = jnp.einsum("bhts,bshd->bthd", weights, group_v, preferred_element_type=jnp.float32)

    tail = jnp.exp(cumulative[:, :, -1:] - cumulative)
    scaled_k = group_k.astype(jnp.float32) * jnp.transpose(tail, (0, 2, 1))[:, :, :, None]
    local_states = jnp.einsum(
        "bshd,bshe->bhde", scaled_k, group_v.astype(jnp.float32), precision=highest
    )
    block_total = jnp.exp(cumulative[:, :, -1])

    run = jnp.zeros((quarter, hd, hd), jnp.float32)
    lead = jnp.ones((quarter,), jnp.float32)
    inside, leads = [], []
    for b in range(n_sy):
        inside.append(run)
        leads.append(lead)
        run = block_total[b][:, None, None] * run + local_states[b]
        lead = lead * block_total[b]
    group_state, group_span = run, lead

    span_rows = jnp.zeros((16, hd), jnp.float32).at[0:3, :quarter].set(jnp.stack(split3(group_span)))
    piece_packed = jnp.concatenate(
        [group_state.reshape(quarter * hd, hd), span_rows], axis=0
    ).astype(jnp.bfloat16)
    pieces_packed = lax.all_gather(piece_packed, "sz", axis=0)
    pieces = pieces_packed[:, : quarter * hd].astype(jnp.float32).reshape(n_sz, quarter, hd, hd)
    span_parts = pieces_packed[:, quarter * hd : quarter * hd + 3, :quarter].astype(jnp.float32)
    spans = (span_parts[:, 0] + span_parts[:, 1]) + span_parts[:, 2]
    run = jnp.zeros((quarter, hd, hd), jnp.float32)
    entering = [run]
    for g in range(n_sz - 1):
        run = spans[g][:, None, None] * run + pieces[g]
        entering.append(run)
    before = lax.dynamic_index_in_dim(jnp.stack(entering), zi, 0, False)

    carried = jnp.stack(leads)[:, :, None, None] * before[None] + jnp.stack(inside)
    inter = jnp.transpose(jnp.exp(cumulative), (0, 2, 1))[:, :, :, None] * jnp.einsum(
        "bthd,bhde->bthe", group_q.astype(jnp.float32), carried, precision=highest
    )
    total_out = intra + inter
    normed = total_out * lax.rsqrt(jnp.mean(total_out * total_out, axis=3, keepdims=True) + 1e-06)
    att_q = normed.astype(jnp.bfloat16).reshape(n_sy, count, qw)
    home = lax.all_to_all(jnp.stack([mix_q, att_q], axis=1), "sy", 0, 0, tiled=True)
    expert_mix = home[:, 0].transpose(1, 0, 2).reshape(count, width)
    attended = home[:, 1].transpose(1, 0, 2).reshape(count, heads * hd)
    return (expert_mix, attended)


def solution(mesh):
    n_dp = mesh.shape["dp"]
    n_seq = mesh.shape["seq"]
    inner = Mesh(mesh.devices.reshape(n_dp, n_seq // GROUP, GROUP), ("dp", "sz", "sy"))
    rows = ("dp", "sz", "sy")
    in_specs = (
        P(rows, None),
        P(rows, None),
        P(),
        P(("sz", "sy"), None, None),
        P(("sz", "sy"), None, None),
        P(("sz", "sy"), None, None),
        P(("sz", "sy"), None),
        P(rows, None),
        P(rows, None),
        P(None, rows),
    )
    out_specs = (P(rows, None), P(rows, None))
    return jax.shard_map(body, mesh=inner, in_specs=in_specs, out_specs=out_specs, check_vma=False)
```

```python
import jax
import jax.numpy as jnp
from jax import lax
from jax.sharding import Mesh
from jax.sharding import PartitionSpec as P

SLOTS = 16
GROUP = 4


def expert_apply(token_rows, gate_matrix, up_matrix, down_matrix, levels):
    gate_values = jnp.dot(token_rows, gate_matrix, preferred_element_type=jnp.float32)
    up_values = jnp.dot(token_rows, up_matrix, preferred_element_type=jnp.float32)
    hidden = jax.nn.silu(gate_values) * up_values
    threshold = 0.125 * levels.astype(jnp.float32)
    spikes = (threshold * jnp.tanh(hidden / threshold)).astype(jnp.bfloat16)
    return jnp.dot(spikes, down_matrix, preferred_element_type=jnp.float32).astype(jnp.bfloat16)


def split3(values):
    hi = lax.reduce_precision(values, exponent_bits=8, mantissa_bits=7)
    rest = values - hi
    mid = lax.reduce_precision(rest, exponent_bits=8, mantissa_bits=7)
    return [hi, mid, rest - mid]


def body(
    tokens, expert_ids, router, w_gate, w_up, w_down, spike_level, queries, key_vectors, log_decay
):
    highest = lax.Precision.HIGHEST
    seq_axes = ("sz", "sy")
    count, width = tokens.shape
    n_experts = router.shape[1]
    heads = log_decay.shape[0]
    hd = queries.shape[1] // heads
    n_sz = lax.axis_size("sz")
    n_sy = lax.axis_size("sy")
    zi = lax.axis_index("sz")
    quarter = heads // n_sy
    qw = quarter * hd

    logits = jnp.dot(tokens, router, preferred_element_type=jnp.float32)
    matches = (
        expert_ids[:, :, None] == jnp.arange(n_experts, dtype=jnp.int32)[None, None, :]
    ).astype(jnp.float32)
    picked = jnp.sum(logits[:, None, :] * matches, axis=2)
    gate_first = jax.nn.sigmoid(picked[:, 0] - picked[:, 1])
    gate_second = jax.nn.sigmoid(picked[:, 1] - picked[:, 0])

    flat_ids = expert_ids.reshape(-1)
    entries = flat_ids.shape[0]
    one_hot = (flat_ids[:, None] == jnp.arange(n_experts, dtype=jnp.int32)[None, :]).astype(
        jnp.bfloat16
    )
    lower = (
        jnp.arange(entries)[:, None] >= jnp.arange(entries)[None, :]
    ).astype(jnp.bfloat16)
    running = jnp.dot(lower, one_hot, preferred_element_type=jnp.float32)
    slots = (jnp.sum(running * one_hot.astype(jnp.float32), axis=1) - 1.0).astype(jnp.int32)
    dest = flat_ids * SLOTS + slots
    n_rows = n_experts * SLOTS
    select = (jnp.arange(n_rows, dtype=jnp.int32)[:, None] == dest[None, :]).astype(jnp.bfloat16)
    select_tok = select.reshape(n_rows, count, 2).sum(axis=2)
    send = jnp.dot(select_tok, tokens, preferred_element_type=jnp.float32).astype(jnp.bfloat16)

    decay_parts = jnp.concatenate(split3(log_decay.reshape(n_sy, 1, quarter * count)), axis=1)
    slot_pairs = slots.reshape(count, 2).astype(jnp.float32)
    id_pairs = expert_ids.astype(jnp.float32)
    fields = [id_pairs[:, 0], slot_pairs[:, 0], id_pairs[:, 1], slot_pairs[:, 1]]
    fields += split3(gate_first) + split3(gate_second)
    n_fields = len(fields)
    info_rows = -(-(n_fields * count) // qw)
    info = jnp.stack(fields).reshape(-1)
    info = jnp.pad(info, (0, info_rows * qw - n_fields * count)).reshape(1, info_rows, qw)
    info = jnp.broadcast_to(info, (n_sy, info_rows, qw))
    q_split = queries.reshape(count, n_sy, qw).transpose(1, 0, 2)
    k_split = key_vectors.reshape(count, n_sy, qw).transpose(1, 0, 2)
    used = 2 * count + 3 + info_rows
    packed = jnp.concatenate(
        [
            q_split,
            k_split,
            decay_parts.astype(jnp.bfloat16),
            info.astype(jnp.bfloat16),
            jnp.zeros((n_sy, (-used) % 16, qw), jnp.bfloat16),
        ],
        axis=1,
    )
    got = lax.all_to_all(packed, "sy", 0, 0, tiled=True)
    group_q = got[:, :count].reshape(n_sy, count, quarter, hd)
    group_k = got[:, count : 2 * count].reshape(n_sy, count, quarter, hd)
    parts = got[:, 2 * count : 2 * count + 3].astype(jnp.float32)
    group_decay = (parts[:, 0] + parts[:, 1] + parts[:, 2]).reshape(n_sy, quarter, count)
    got_info = got[:, 2 * count + 3 : used].astype(jnp.float32).reshape(n_sy, info_rows * qw)
    got_info = got_info[:, : n_fields * count].reshape(n_sy, n_fields, count)
    g_first = (got_info[:, 4] + got_info[:, 5]) + got_info[:, 6]
    g_second = (got_info[:, 7] + got_info[:, 8]) + got_info[:, 9]
    row_first = (got_info[:, 0] * SLOTS + got_info[:, 1]).astype(jnp.int32)
    row_second = (got_info[:, 2] * SLOTS + got_info[:, 3]).astype(jnp.int32)

    recv = lax.all_to_all(send.reshape(n_experts, SLOTS, width), seq_axes, 0, 0, tiled=True)
    computed = expert_apply(
        recv.reshape(n_rows, width), w_gate[0], w_up[0], w_down[0], spike_level[0]
    )
    outgoing = computed.reshape(n_sz, n_sy, SLOTS, n_sy, qw).transpose(0, 3, 1, 2, 4)
    outgoing = outgoing.reshape(n_sz * n_sy, n_sy * SLOTS, qw)
    back = lax.all_to_all(outgoing, seq_axes, 0, 0, tiled=True)
    table = back.reshape(n_experts, n_sy, SLOTS, qw)
    lanes_e = jnp.arange(n_experts, dtype=jnp.int32)[None, None, :, None]
    lanes_s = jnp.arange(SLOTS, dtype=jnp.int32)[None, None, None, :]

    def pick(row):
        e = (row // SLOTS)[:, :, None, None]
        s = (row % SLOTS)[:, :, None, None]
        return ((e == lanes_e) & (s == lanes_s)).astype(jnp.bfloat16)

    first_out = jnp.einsum(
        "btes,ebsc->btc", pick(row_first), table, preferred_element_type=jnp.float32
    )
    second_out = jnp.einsum(
        "btes,ebsc->btc", pick(row_second), table, preferred_element_type=jnp.float32
    )
    mix_q = (g_first[:, :, None] * first_out + g_second[:, :, None] * second_out).astype(
        jnp.bfloat16
    )

    group_v = mix_q.reshape(n_sy, count, quarter, hd)
    cumulative = jnp.cumsum(group_decay, axis=2)
    scores = jnp.einsum(
        "bthd,bshd->bhts", group_q, group_k, preferred_element_type=jnp.float32
    )
    causal = jnp.arange(count)[:, None] >= jnp.arange(count)[None, :]
    spread = cumulative[:, :, :, None] - cumulative[:, :, None, :]
    decay = jnp.where(causal[None, None], jnp.exp(jnp.minimum(spread, 0.0)), 0.0)
    weights = (scores * decay).astype(jnp.bfloat16)
    intra = jnp.einsum("bhts,bshd->bthd", weights, group_v, preferred_element_type=jnp.float32)

    tail = jnp.exp(cumulative[:, :, -1:] - cumulative)
    scaled_k = group_k.astype(jnp.float32) * jnp.transpose(tail, (0, 2, 1))[:, :, :, None]
    local_states = jnp.einsum(
        "bshd,bshe->bhde", scaled_k, group_v.astype(jnp.float32), precision=highest
    )
    block_total = jnp.exp(cumulative[:, :, -1])

    run = jnp.zeros((quarter, hd, hd), jnp.float32)
    lead = jnp.ones((quarter,), jnp.float32)
    inside, leads = [], []
    for b in range(n_sy):
        inside.append(run)
        leads.append(lead)
        run = block_total[b][:, None, None] * run + local_states[b]
        lead = lead * block_total[b]
    group_state, group_span = run, lead

    span_rows = jnp.zeros((8, hd), jnp.float32).at[0, :quarter].set(group_span)
    piece_packed = jnp.concatenate([group_state.reshape(quarter * hd, hd), span_rows], axis=0)
    pieces_packed = lax.all_gather(piece_packed, "sz", axis=0)
    pieces = pieces_packed[:, : quarter * hd].reshape(n_sz, quarter, hd, hd)
    spans = pieces_packed[:, quarter * hd, :quarter]
    run = jnp.zeros((quarter, hd, hd), jnp.float32)
    entering = [run]
    for g in range(n_sz - 1):
        run = spans[g][:, None, None] * run + pieces[g]
        entering.append(run)
    before = lax.dynamic_index_in_dim(jnp.stack(entering), zi, 0, False)

    carried = jnp.stack(leads)[:, :, None, None] * before[None] + jnp.stack(inside)
    inter = jnp.transpose(jnp.exp(cumulative), (0, 2, 1))[:, :, :, None] * jnp.einsum(
        "bthd,bhde->bthe", group_q.astype(jnp.float32), carried, precision=highest
    )
    total_out = intra + inter
    normed = total_out * lax.rsqrt(jnp.mean(total_out * total_out, axis=3, keepdims=True) + 1e-06)
    att_q = normed.astype(jnp.bfloat16).reshape(n_sy, count, qw)
    home = lax.all_to_all(jnp.stack([mix_q, att_q], axis=1), "sy", 0, 0, tiled=True)
    expert_mix = home[:, 0].transpose(1, 0, 2).reshape(count, width)
    attended = home[:, 1].transpose(1, 0, 2).reshape(count, heads * hd)
    return (expert_mix, attended)


def solution(mesh):
    n_dp = mesh.shape["dp"]
    n_seq = mesh.shape["seq"]
    inner = Mesh(mesh.devices.reshape(n_dp, n_seq // GROUP, GROUP), ("dp", "sz", "sy"))
    rows = ("dp", "sz", "sy")
    in_specs = (
        P(rows, None),
        P(rows, None),
        P(),
        P(("sz", "sy"), None, None),
        P(("sz", "sy"), None, None),
        P(("sz", "sy"), None, None),
        P(("sz", "sy"), None),
        P(rows, None),
        P(rows, None),
        P(None, rows),
    )
    out_specs = (P(rows, None), P(rows, None))
    return jax.shard_map(body, mesh=inner, in_specs=in_specs, out_specs=out_specs, check_vma=False)
```

```python
import jax
import jax.numpy as jnp
from jax import lax
from jax.sharding import Mesh
from jax.sharding import PartitionSpec as P

SLOTS = 16
GROUP = 4


def expert_apply(token_rows, gate_matrix, up_matrix, down_matrix, levels):
    gate_values = jnp.dot(token_rows, gate_matrix, preferred_element_type=jnp.float32)
    up_values = jnp.dot(token_rows, up_matrix, preferred_element_type=jnp.float32)
    hidden = jax.nn.silu(gate_values) * up_values
    threshold = 0.125 * levels.astype(jnp.float32)
    spikes = (threshold * jnp.tanh(hidden / threshold)).astype(jnp.bfloat16)
    return jnp.dot(spikes, down_matrix, preferred_element_type=jnp.float32).astype(jnp.bfloat16)


def split3(values):
    hi = lax.reduce_precision(values, exponent_bits=8, mantissa_bits=7)
    rest = values - hi
    mid = lax.reduce_precision(rest, exponent_bits=8, mantissa_bits=7)
    return [hi, mid, rest - mid]


def body(
    tokens, expert_ids, router, w_gate, w_up, w_down, spike_level, queries, key_vectors, log_decay
):
    highest = lax.Precision.HIGHEST
    seq_axes = ("sz", "sy")
    count, width = tokens.shape
    n_experts = router.shape[1]
    heads = log_decay.shape[0]
    hd = queries.shape[1] // heads
    n_sz = lax.axis_size("sz")
    n_sy = lax.axis_size("sy")
    zi = lax.axis_index("sz")
    quarter = heads // n_sy
    qw = quarter * hd

    logits = jnp.dot(tokens, router, preferred_element_type=jnp.float32)
    matches = (
        expert_ids[:, :, None] == jnp.arange(n_experts, dtype=jnp.int32)[None, None, :]
    ).astype(jnp.float32)
    picked = jnp.sum(logits[:, None, :] * matches, axis=2)
    gate_first = jax.nn.sigmoid(picked[:, 0] - picked[:, 1])
    gate_second = jax.nn.sigmoid(picked[:, 1] - picked[:, 0])

    flat_ids = expert_ids.reshape(-1)
    entries = flat_ids.shape[0]
    one_hot = (flat_ids[:, None] == jnp.arange(n_experts, dtype=jnp.int32)[None, :]).astype(
        jnp.bfloat16
    )
    lower = (
        jnp.arange(entries)[:, None] >= jnp.arange(entries)[None, :]
    ).astype(jnp.bfloat16)
    running = jnp.dot(lower, one_hot, preferred_element_type=jnp.float32)
    slots = (jnp.sum(running * one_hot.astype(jnp.float32), axis=1) - 1.0).astype(jnp.int32)
    dest = flat_ids * SLOTS + slots
    n_rows = n_experts * SLOTS
    select = (jnp.arange(n_rows, dtype=jnp.int32)[:, None] == dest[None, :]).astype(jnp.bfloat16)
    select_tok = select.reshape(n_rows, count, 2).sum(axis=2)
    send = jnp.dot(select_tok, tokens, preferred_element_type=jnp.float32).astype(jnp.bfloat16)

    decay_parts = jnp.concatenate(split3(log_decay.reshape(n_sy, 1, quarter * count)), axis=1)
    slot_pairs = slots.reshape(count, 2).astype(jnp.float32)
    id_pairs = expert_ids.astype(jnp.float32)
    fields = [id_pairs[:, 0], slot_pairs[:, 0], id_pairs[:, 1], slot_pairs[:, 1]]
    fields += split3(gate_first) + split3(gate_second)
    n_fields = len(fields)
    info_rows = -(-(n_fields * count) // qw)
    info = jnp.stack(fields).reshape(-1)
    info = jnp.pad(info, (0, info_rows * qw - n_fields * count)).reshape(1, info_rows, qw)
    info = jnp.broadcast_to(info, (n_sy, info_rows, qw))
    q_split = queries.reshape(count, n_sy, qw).transpose(1, 0, 2)
    k_split = key_vectors.reshape(count, n_sy, qw).transpose(1, 0, 2)
    used = 2 * count + 3 + info_rows
    packed = jnp.concatenate(
        [
            q_split,
            k_split,
            decay_parts.astype(jnp.bfloat16),
            info.astype(jnp.bfloat16),
            jnp.zeros((n_sy, (-used) % 16, qw), jnp.bfloat16),
        ],
        axis=1,
    )
    got = lax.all_to_all(packed, "sy", 0, 0, tiled=True)
    group_q = got[:, :count].reshape(n_sy, count, quarter, hd)
    group_k = got[:, count : 2 * count].reshape(n_sy, count, quarter, hd)
    parts = got[:, 2 * count : 2 * count + 3].astype(jnp.float32)
    group_decay = (parts[:, 0] + parts[:, 1] + parts[:, 2]).reshape(n_sy, quarter, count)
    got_info = got[:, 2 * count + 3 : used].astype(jnp.float32).reshape(n_sy, info_rows * qw)
    got_info = got_info[:, : n_fields * count].reshape(n_sy, n_fields, count)
    g_first = (got_info[:, 4] + got_info[:, 5]) + got_info[:, 6]
    g_second = (got_info[:, 7] + got_info[:, 8]) + got_info[:, 9]
    row_first = (got_info[:, 0] * SLOTS + got_info[:, 1]).astype(jnp.int32)
    row_second = (got_info[:, 2] * SLOTS + got_info[:, 3]).astype(jnp.int32)

    recv = lax.all_to_all(send.reshape(n_experts, SLOTS, width), seq_axes, 0, 0, tiled=True)
    computed = expert_apply(
        recv.reshape(n_rows, width), w_gate[0], w_up[0], w_down[0], spike_level[0]
    )
    outgoing = computed.reshape(n_sz, n_sy, SLOTS, n_sy, qw).transpose(0, 3, 1, 2, 4)
    outgoing = outgoing.reshape(n_sz * n_sy, n_sy * SLOTS, qw)
    back = lax.all_to_all(outgoing, seq_axes, 0, 0, tiled=True)
    table = back.reshape(n_experts, n_sy, SLOTS, qw)
    lanes_e = jnp.arange(n_experts, dtype=jnp.int32)[None, None, :, None]
    lanes_s = jnp.arange(SLOTS, dtype=jnp.int32)[None, None, None, :]

    def pick(row):
        e = (row // SLOTS)[:, :, None, None]
        s = (row % SLOTS)[:, :, None, None]
        return ((e == lanes_e) & (s == lanes_s)).astype(jnp.bfloat16)

    first_out = jnp.einsum(
        "btes,ebsc->btc", pick(row_first), table, preferred_element_type=jnp.float32
    )
    second_out = jnp.einsum(
        "btes,ebsc->btc", pick(row_second), table, preferred_element_type=jnp.float32
    )
    mix_q = (g_first[:, :, None] * first_out + g_second[:, :, None] * second_out).astype(
        jnp.bfloat16
    )

    group_v = mix_q.reshape(n_sy, count, quarter, hd)
    cumulative = jnp.cumsum(group_decay, axis=2)
    scores = jnp.einsum(
        "bthd,bshd->bhts", group_q, group_k, preferred_element_type=jnp.float32
    )
    causal = jnp.arange(count)[:, None] >= jnp.arange(count)[None, :]
    spread = cumulative[:, :, :, None] - cumulative[:, :, None, :]
    decay = jnp.where(causal[None, None], jnp.exp(jnp.minimum(spread, 0.0)), 0.0)
    weights = (scores * decay).astype(jnp.bfloat16)
    intra = jnp.einsum("bhts,bshd->bthd", weights, group_v, preferred_element_type=jnp.float32)

    tail = jnp.exp(cumulative[:, :, -1:] - cumulative)
    scaled_k = group_k.astype(jnp.float32) * jnp.transpose(tail, (0, 2, 1))[:, :, :, None]
    local_states = jnp.einsum(
        "bshd,bshe->bhde", scaled_k, group_v.astype(jnp.float32), precision=highest
    )
    block_total = jnp.exp(cumulative[:, :, -1])

    run = jnp.zeros((quarter, hd, hd), jnp.float32)
    lead = jnp.ones((quarter,), jnp.float32)
    inside, leads = [], []
    for b in range(n_sy):
        inside.append(run)
        leads.append(lead)
        run = block_total[b][:, None, None] * run + local_states[b]
        lead = lead * block_total[b]
    group_state, group_span = run, lead

    def shifted(value, span, by):
        pairs = [(i, i + by) for i in range(n_sz - by)]
        got_value = lax.ppermute(value, "sz", pairs)
        got_span = lax.ppermute(span, "sz", pairs)
        return got_value, jnp.where(zi >= by, got_span, 1.0)

    def join(earlier, later):
        (v_e, s_e), (v_l, s_l) = earlier, later
        return (s_l[:, None, None] * v_e + v_l, s_e * s_l)

    one = shifted(group_state, group_span, 1)
    two = shifted(group_state, group_span, 2)
    window = join(two, one)
    reach = 2
    while reach < n_sz:
        window = join(shifted(window[0], window[1], reach), window)
        reach *= 2
    before = window[0]

    carried = jnp.stack(leads)[:, :, None, None] * before[None] + jnp.stack(inside)
    inter = jnp.transpose(jnp.exp(cumulative), (0, 2, 1))[:, :, :, None] * jnp.einsum(
        "bthd,bhde->bthe", group_q.astype(jnp.float32), carried, precision=highest
    )
    total_out = intra + inter
    normed = total_out * lax.rsqrt(jnp.mean(total_out * total_out, axis=3, keepdims=True) + 1e-06)
    att_q = normed.astype(jnp.bfloat16).reshape(n_sy, count, qw)
    home = lax.all_to_all(jnp.stack([mix_q, att_q], axis=1), "sy", 0, 0, tiled=True)
    expert_mix = home[:, 0].transpose(1, 0, 2).reshape(count, width)
    attended = home[:, 1].transpose(1, 0, 2).reshape(count, heads * hd)
    return (expert_mix, attended)


def solution(mesh):
    n_dp = mesh.shape["dp"]
    n_seq = mesh.shape["seq"]
    inner = Mesh(mesh.devices.reshape(n_dp, n_seq // GROUP, GROUP), ("dp", "sz", "sy"))
    rows = ("dp", "sz", "sy")
    in_specs = (
        P(rows, None),
        P(rows, None),
        P(),
        P(("sz", "sy"), None, None),
        P(("sz", "sy"), None, None),
        P(("sz", "sy"), None, None),
        P(("sz", "sy"), None),
        P(rows, None),
        P(rows, None),
        P(None, rows),
    )
    out_specs = (P(rows, None), P(rows, None))
    return jax.shard_map(body, mesh=inner, in_specs=in_specs, out_specs=out_specs, check_vma=False)
```

```python
import jax
import jax.numpy as jnp
from jax import lax
from jax.sharding import Mesh
from jax.sharding import PartitionSpec as P

SLOTS = 16
GROUP = 4


def expert_spikes(token_rows, gate_matrix, up_matrix, levels):
    gate_values = jnp.dot(token_rows, gate_matrix, preferred_element_type=jnp.float32)
    up_values = jnp.dot(token_rows, up_matrix, preferred_element_type=jnp.float32)
    hidden = jax.nn.silu(gate_values) * up_values
    threshold = 0.125 * levels.astype(jnp.float32)
    return (threshold * jnp.tanh(hidden / threshold)).astype(jnp.bfloat16)


def split3(values):
    hi = lax.reduce_precision(values, exponent_bits=8, mantissa_bits=7)
    rest = values - hi
    mid = lax.reduce_precision(rest, exponent_bits=8, mantissa_bits=7)
    return [hi, mid, rest - mid]


def body(
    tokens, expert_ids, router, w_gate, w_up, w_down, spike_level, queries, key_vectors, log_decay
):
    highest = lax.Precision.HIGHEST
    seq_axes = ("sz", "sy")
    count, width = tokens.shape
    n_experts = router.shape[1]
    heads = log_decay.shape[0]
    hd = queries.shape[1] // heads
    n_sz = lax.axis_size("sz")
    n_sy = lax.axis_size("sy")
    zi = lax.axis_index("sz")
    quarter = heads // n_sy
    qw = quarter * hd

    logits = jnp.dot(tokens, router, preferred_element_type=jnp.float32)
    matches = (
        expert_ids[:, :, None] == jnp.arange(n_experts, dtype=jnp.int32)[None, None, :]
    ).astype(jnp.float32)
    picked = jnp.sum(logits[:, None, :] * matches, axis=2)
    gate_first = jax.nn.sigmoid(picked[:, 0] - picked[:, 1])
    gate_second = jax.nn.sigmoid(picked[:, 1] - picked[:, 0])

    flat_ids = expert_ids.reshape(-1)
    entries = flat_ids.shape[0]
    one_hot = (flat_ids[:, None] == jnp.arange(n_experts, dtype=jnp.int32)[None, :]).astype(
        jnp.bfloat16
    )
    lower = (
        jnp.arange(entries)[:, None] >= jnp.arange(entries)[None, :]
    ).astype(jnp.bfloat16)
    running = jnp.dot(lower, one_hot, preferred_element_type=jnp.float32)
    slots = (jnp.sum(running * one_hot.astype(jnp.float32), axis=1) - 1.0).astype(jnp.int32)
    dest = flat_ids * SLOTS + slots
    n_rows = n_experts * SLOTS
    select = (jnp.arange(n_rows, dtype=jnp.int32)[:, None] == dest[None, :]).astype(jnp.bfloat16)
    select_tok = select.reshape(n_rows, count, 2).sum(axis=2)
    send = jnp.dot(select_tok, tokens, preferred_element_type=jnp.float32).astype(jnp.bfloat16)

    decay_parts = jnp.concatenate(split3(log_decay.reshape(n_sy, 1, quarter * count)), axis=1)
    slot_pairs = slots.reshape(count, 2).astype(jnp.float32)
    id_pairs = expert_ids.astype(jnp.float32)
    fields = [id_pairs[:, 0], slot_pairs[:, 0], id_pairs[:, 1], slot_pairs[:, 1]]
    fields += split3(gate_first) + split3(gate_second)
    n_fields = len(fields)
    info_rows = -(-(n_fields * count) // qw)
    info = jnp.stack(fields).reshape(-1)
    info = jnp.pad(info, (0, info_rows * qw - n_fields * count)).reshape(1, info_rows, qw)
    info = jnp.broadcast_to(info, (n_sy, info_rows, qw))
    q_split = queries.reshape(count, n_sy, qw).transpose(1, 0, 2)
    k_split = key_vectors.reshape(count, n_sy, qw).transpose(1, 0, 2)
    used = 2 * count + 3 + info_rows
    packed = jnp.concatenate(
        [
            q_split,
            k_split,
            decay_parts.astype(jnp.bfloat16),
            info.astype(jnp.bfloat16),
            jnp.zeros((n_sy, (-used) % 16, qw), jnp.bfloat16),
        ],
        axis=1,
    )
    got = lax.all_to_all(packed, "sy", 0, 0, tiled=True)
    group_q = got[:, :count].reshape(n_sy, count, quarter, hd)
    group_k = got[:, count : 2 * count].reshape(n_sy, count, quarter, hd)
    parts = got[:, 2 * count : 2 * count + 3].astype(jnp.float32)
    group_decay = (parts[:, 0] + parts[:, 1] + parts[:, 2]).reshape(n_sy, quarter, count)
    got_info = got[:, 2 * count + 3 : used].astype(jnp.float32).reshape(n_sy, info_rows * qw)
    got_info = got_info[:, : n_fields * count].reshape(n_sy, n_fields, count)
    g_first = (got_info[:, 4] + got_info[:, 5]) + got_info[:, 6]
    g_second = (got_info[:, 7] + got_info[:, 8]) + got_info[:, 9]
    row_first = (got_info[:, 0] * SLOTS + got_info[:, 1]).astype(jnp.int32)
    row_second = (got_info[:, 2] * SLOTS + got_info[:, 3]).astype(jnp.int32)

    recv = lax.all_to_all(send.reshape(n_experts, SLOTS, width), seq_axes, 0, 0, tiled=True)
    spikes = expert_spikes(recv.reshape(n_rows, width), w_gate[0], w_up[0], spike_level[0])
    outgoing = jnp.einsum(
        "zrk,kjc->zjrc",
        spikes.reshape(n_sz, n_sy * SLOTS, -1),
        w_down[0].reshape(-1, n_sy, qw),
        preferred_element_type=jnp.float32,
    ).astype(jnp.bfloat16)
    outgoing = outgoing.reshape(n_sz * n_sy, n_sy * SLOTS, qw)
    back = lax.all_to_all(outgoing, seq_axes, 0, 0, tiled=True)
    table = back.reshape(n_experts, n_sy, SLOTS, qw)
    lanes_e = jnp.arange(n_experts, dtype=jnp.int32)[None, None, :, None]
    lanes_s = jnp.arange(SLOTS, dtype=jnp.int32)[None, None, None, :]

    def pick(row):
        e = (row // SLOTS)[:, :, None, None]
        s = (row % SLOTS)[:, :, None, None]
        return ((e == lanes_e) & (s == lanes_s)).astype(jnp.bfloat16)

    first_out = jnp.einsum(
        "btes,ebsc->btc", pick(row_first), table, preferred_element_type=jnp.float32
    )
    second_out = jnp.einsum(
        "btes,ebsc->btc", pick(row_second), table, preferred_element_type=jnp.float32
    )
    mix_q = (g_first[:, :, None] * first_out + g_second[:, :, None] * second_out).astype(
        jnp.bfloat16
    )

    group_v = mix_q.reshape(n_sy, count, quarter, hd)
    cumulative = jnp.cumsum(group_decay, axis=2)
    scores = jnp.einsum(
        "bthd,bshd->bhts", group_q, group_k, preferred_element_type=jnp.float32
    )
    causal = jnp.arange(count)[:, None] >= jnp.arange(count)[None, :]
    spread = cumulative[:, :, :, None] - cumulative[:, :, None, :]
    decay = jnp.where(causal[None, None], jnp.exp(jnp.minimum(spread, 0.0)), 0.0)
    weights = (scores * decay).astype(jnp.bfloat16)
    intra = jnp.einsum("bhts,bshd->bthd", weights, group_v, preferred_element_type=jnp.float32)

    tail = jnp.exp(cumulative[:, :, -1:] - cumulative)
    scaled_k = group_k.astype(jnp.float32) * jnp.transpose(tail, (0, 2, 1))[:, :, :, None]
    local_states = jnp.einsum(
        "bshd,bshe->bhde", scaled_k, group_v.astype(jnp.float32), precision=highest
    )
    block_total = jnp.exp(cumulative[:, :, -1])

    run = jnp.zeros((quarter, hd, hd), jnp.float32)
    lead = jnp.ones((quarter,), jnp.float32)
    inside, leads = [], []
    for b in range(n_sy):
        inside.append(run)
        leads.append(lead)
        run = block_total[b][:, None, None] * run + local_states[b]
        lead = lead * block_total[b]
    group_state, group_span = run, lead

    def shifted(value, span, by):
        pairs = [(i, i + by) for i in range(n_sz - by)]
        got_value = lax.ppermute(value, "sz", pairs)
        got_span = lax.ppermute(span, "sz", pairs)
        return got_value, jnp.where(zi >= by, got_span, 1.0)

    def join(earlier, later):
        (v_e, s_e), (v_l, s_l) = earlier, later
        return (s_l[:, None, None] * v_e + v_l, s_e * s_l)

    one = shifted(group_state, group_span, 1)
    two = shifted(group_state, group_span, 2)
    window = join(two, one)
    reach = 2
    while reach < n_sz:
        window = join(shifted(window[0], window[1], reach), window)
        reach *= 2
    before = window[0]

    carried = jnp.stack(leads)[:, :, None, None] * before[None] + jnp.stack(inside)
    inter = jnp.transpose(jnp.exp(cumulative), (0, 2, 1))[:, :, :, None] * jnp.einsum(
        "bthd,bhde->bthe", group_q.astype(jnp.float32), carried, precision=highest
    )
    total_out = intra + inter
    normed = total_out * lax.rsqrt(jnp.mean(total_out * total_out, axis=3, keepdims=True) + 1e-06)
    att_q = normed.astype(jnp.bfloat16).reshape(n_sy, count, qw)
    home = lax.all_to_all(jnp.stack([mix_q, att_q], axis=1), "sy", 0, 3, tiled=True)
    expert_mix = home[0, 0]
    attended = home[0, 1]
    return (expert_mix, attended)


def solution(mesh):
    n_dp = mesh.shape["dp"]
    n_seq = mesh.shape["seq"]
    inner = Mesh(mesh.devices.reshape(n_dp, n_seq // GROUP, GROUP), ("dp", "sz", "sy"))
    rows = ("dp", "sz", "sy")
    in_specs = (
        P(rows, None),
        P(rows, None),
        P(),
        P(("sz", "sy"), None, None),
        P(("sz", "sy"), None, None),
        P(("sz", "sy"), None, None),
        P(("sz", "sy"), None),
        P(rows, None),
        P(rows, None),
        P(None, rows),
    )
    out_specs = (P(rows, None), P(rows, None))
    return jax.shard_map(body, mesh=inner, in_specs=in_specs, out_specs=out_specs, check_vma=False)
```

```python
import jax
import jax.numpy as jnp
from jax import lax
from jax.sharding import Mesh
from jax.sharding import PartitionSpec as P

SLOTS = 16
GROUP = 4


def expert_spikes(token_rows, gate_matrix, up_matrix, levels):
    gate_values = jnp.dot(token_rows, gate_matrix, preferred_element_type=jnp.float32)
    up_values = jnp.dot(token_rows, up_matrix, preferred_element_type=jnp.float32)
    hidden = jax.nn.silu(gate_values) * up_values
    threshold = 0.125 * levels.astype(jnp.float32)
    return (threshold * jnp.tanh(hidden / threshold)).astype(jnp.bfloat16)


def split3(values):
    hi = lax.reduce_precision(values, exponent_bits=8, mantissa_bits=7)
    rest = values - hi
    mid = lax.reduce_precision(rest, exponent_bits=8, mantissa_bits=7)
    return [hi, mid, rest - mid]


def body(
    tokens, expert_ids, router, w_gate, w_up, w_down, spike_level, queries, key_vectors, log_decay
):
    highest = lax.Precision.HIGHEST
    seq_axes = ("sz", "sy")
    count, width = tokens.shape
    n_experts = router.shape[1]
    heads = log_decay.shape[0]
    hd = queries.shape[1] // heads
    n_sz = lax.axis_size("sz")
    n_sy = lax.axis_size("sy")
    zi = lax.axis_index("sz")
    quarter = heads // n_sy
    qw = quarter * hd

    logits = jnp.dot(tokens, router, preferred_element_type=jnp.float32)
    matches = (
        expert_ids[:, :, None] == jnp.arange(n_experts, dtype=jnp.int32)[None, None, :]
    ).astype(jnp.float32)
    picked = jnp.sum(logits[:, None, :] * matches, axis=2)
    gate_first = jax.nn.sigmoid(picked[:, 0] - picked[:, 1])
    gate_second = jax.nn.sigmoid(picked[:, 1] - picked[:, 0])

    flat_ids = expert_ids.reshape(-1)
    entries = flat_ids.shape[0]
    one_hot = (flat_ids[:, None] == jnp.arange(n_experts, dtype=jnp.int32)[None, :]).astype(
        jnp.bfloat16
    )
    lower = (
        jnp.arange(entries)[:, None] >= jnp.arange(entries)[None, :]
    ).astype(jnp.bfloat16)
    running = jnp.dot(lower, one_hot, preferred_element_type=jnp.float32)
    slots = (jnp.sum(running * one_hot.astype(jnp.float32), axis=1) - 1.0).astype(jnp.int32)
    dest = flat_ids * SLOTS + slots
    n_rows = n_experts * SLOTS
    select = (jnp.arange(n_rows, dtype=jnp.int32)[:, None] == dest[None, :]).astype(jnp.bfloat16)
    select_tok = select.reshape(n_rows, count, 2).sum(axis=2)
    send = jnp.dot(select_tok, tokens, preferred_element_type=jnp.float32).astype(jnp.bfloat16)

    decay_parts = jnp.concatenate(split3(log_decay.reshape(n_sy, 1, quarter * count)), axis=1)
    slot_pairs = slots.reshape(count, 2).astype(jnp.float32)
    id_pairs = expert_ids.astype(jnp.float32)
    fields = [id_pairs[:, 0], slot_pairs[:, 0], id_pairs[:, 1], slot_pairs[:, 1]]
    fields += split3(gate_first) + split3(gate_second)
    n_fields = len(fields)
    info_rows = -(-(n_fields * count) // qw)
    info = jnp.stack(fields).reshape(-1)
    info = jnp.pad(info, (0, info_rows * qw - n_fields * count)).reshape(1, info_rows, qw)
    info = jnp.broadcast_to(info, (n_sy, info_rows, qw))
    q_split = queries.reshape(count, n_sy, qw).transpose(1, 0, 2)
    k_split = key_vectors.reshape(count, n_sy, qw).transpose(1, 0, 2)
    used = 2 * count + 3 + info_rows
    packed = jnp.concatenate(
        [
            q_split,
            k_split,
            decay_parts.astype(jnp.bfloat16),
            info.astype(jnp.bfloat16),
            jnp.zeros((n_sy, (-used) % 16, qw), jnp.bfloat16),
        ],
        axis=1,
    )
    got = lax.all_to_all(packed, "sy", 0, 0, tiled=True)
    group_q = got[:, :count].reshape(n_sy, count, quarter, hd)
    group_k = got[:, count : 2 * count].reshape(n_sy, count, quarter, hd)
    parts = got[:, 2 * count : 2 * count + 3].astype(jnp.float32)
    group_decay = (parts[:, 0] + parts[:, 1] + parts[:, 2]).reshape(n_sy, quarter, count)
    got_info = got[:, 2 * count + 3 : used].astype(jnp.float32).reshape(n_sy, info_rows * qw)
    got_info = got_info[:, : n_fields * count].reshape(n_sy, n_fields, count)
    g_first = (got_info[:, 4] + got_info[:, 5]) + got_info[:, 6]
    g_second = (got_info[:, 7] + got_info[:, 8]) + got_info[:, 9]
    row_first = (got_info[:, 0] * SLOTS + got_info[:, 1]).astype(jnp.int32)
    row_second = (got_info[:, 2] * SLOTS + got_info[:, 3]).astype(jnp.int32)

    recv = lax.all_to_all(send.reshape(n_experts, SLOTS, width), seq_axes, 0, 0, tiled=True)
    spikes = expert_spikes(recv.reshape(n_rows, width), w_gate[0], w_up[0], spike_level[0])
    outgoing = jnp.einsum(
        "zrk,kjc->zjrc",
        spikes.reshape(n_sz, n_sy * SLOTS, -1),
        w_down[0].reshape(-1, n_sy, qw),
        preferred_element_type=jnp.float32,
    ).astype(jnp.bfloat16)
    outgoing = outgoing.reshape(n_sz * n_sy, n_sy * SLOTS, qw)
    back = lax.all_to_all(outgoing, seq_axes, 0, 0, tiled=True)
    table = back.reshape(n_experts, n_sy, SLOTS, qw)
    lanes_e = jnp.arange(n_experts, dtype=jnp.int32)[None, None, :, None]
    lanes_s = jnp.arange(SLOTS, dtype=jnp.int32)[None, None, None, :]

    def pick(row):
        e = (row // SLOTS)[:, :, None, None]
        s = (row % SLOTS)[:, :, None, None]
        return ((e == lanes_e) & (s == lanes_s)).astype(jnp.bfloat16)

    first_out = jnp.einsum(
        "btes,ebsc->btc", pick(row_first), table, preferred_element_type=jnp.float32
    )
    second_out = jnp.einsum(
        "btes,ebsc->btc", pick(row_second), table, preferred_element_type=jnp.float32
    )
    mix_q = (g_first[:, :, None] * first_out + g_second[:, :, None] * second_out).astype(
        jnp.bfloat16
    )

    group_v = mix_q.reshape(n_sy, count, quarter, hd)
    cumulative = jnp.cumsum(group_decay, axis=2)
    scores = jnp.einsum(
        "bthd,bshd->bhts", group_q, group_k, preferred_element_type=jnp.float32
    )
    causal = jnp.arange(count)[:, None] >= jnp.arange(count)[None, :]
    spread = cumulative[:, :, :, None] - cumulative[:, :, None, :]
    decay = jnp.where(causal[None, None], jnp.exp(jnp.minimum(spread, 0.0)), 0.0)
    weights = (scores * decay).astype(jnp.bfloat16)
    intra = jnp.einsum("bhts,bshd->bthd", weights, group_v, preferred_element_type=jnp.float32)

    tail = jnp.exp(cumulative[:, :, -1:] - cumulative)
    scaled_k = group_k.astype(jnp.float32) * jnp.transpose(tail, (0, 2, 1))[:, :, :, None]
    local_states = jnp.einsum(
        "bshd,bshe->bhde", scaled_k, group_v.astype(jnp.float32), precision=highest
    )
    block_total = jnp.exp(cumulative[:, :, -1])

    run = jnp.zeros((quarter, hd, hd), jnp.float32)
    lead = jnp.ones((quarter,), jnp.float32)
    inside, leads = [], []
    for b in range(n_sy):
        inside.append(run)
        leads.append(lead)
        run = block_total[b][:, None, None] * run + local_states[b]
        lead = lead * block_total[b]
    group_state, group_span = run, lead

    span_rows = jnp.zeros((8, hd), jnp.float32).at[0, :quarter].set(group_span)
    piece_packed = jnp.concatenate([group_state.reshape(quarter * hd, hd), span_rows], axis=0)
    pieces_packed = lax.all_gather(piece_packed, "sz", axis=0)
    pieces = pieces_packed[:, : quarter * hd].reshape(n_sz, quarter, hd, hd)
    spans = pieces_packed[:, quarter * hd, :quarter]
    run = jnp.zeros((quarter, hd, hd), jnp.float32)
    entering = [run]
    for g in range(n_sz - 1):
        run = spans[g][:, None, None] * run + pieces[g]
        entering.append(run)
    before = lax.dynamic_index_in_dim(jnp.stack(entering), zi, 0, False)

    carried = jnp.stack(leads)[:, :, None, None] * before[None] + jnp.stack(inside)
    inter = jnp.transpose(jnp.exp(cumulative), (0, 2, 1))[:, :, :, None] * jnp.einsum(
        "bthd,bhde->bthe", group_q.astype(jnp.float32), carried, precision=highest
    )
    total_out = intra + inter
    normed = total_out * lax.rsqrt(jnp.mean(total_out * total_out, axis=3, keepdims=True) + 1e-06)
    att_q = normed.astype(jnp.bfloat16).reshape(n_sy, count, qw)
    home = lax.all_to_all(jnp.stack([mix_q, att_q], axis=1), "sy", 0, 3, tiled=True)
    expert_mix = home[0, 0]
    attended = home[0, 1]
    return (expert_mix, attended)


def solution(mesh):
    n_dp = mesh.shape["dp"]
    n_seq = mesh.shape["seq"]
    inner = Mesh(mesh.devices.reshape(n_dp, n_seq // GROUP, GROUP), ("dp", "sz", "sy"))
    rows = ("dp", "sz", "sy")
    in_specs = (
        P(rows, None),
        P(rows, None),
        P(),
        P(("sz", "sy"), None, None),
        P(("sz", "sy"), None, None),
        P(("sz", "sy"), None, None),
        P(("sz", "sy"), None),
        P(rows, None),
        P(rows, None),
        P(None, rows),
    )
    out_specs = (P(rows, None), P(rows, None))
    return jax.shard_map(body, mesh=inner, in_specs=in_specs, out_specs=out_specs, check_vma=False)
```

```python
import jax
import jax.numpy as jnp
from jax import lax
from jax.sharding import Mesh
from jax.sharding import PartitionSpec as P

SLOTS = 16
GROUP = 4


def expert_spikes(token_rows, gate_matrix, up_matrix, levels):
    gate_values = jnp.dot(token_rows, gate_matrix, preferred_element_type=jnp.float32)
    up_values = jnp.dot(token_rows, up_matrix, preferred_element_type=jnp.float32)
    hidden = jax.nn.silu(gate_values) * up_values
    threshold = 0.125 * levels.astype(jnp.float32)
    return (threshold * jnp.tanh(hidden / threshold)).astype(jnp.bfloat16)


def split3(values):
    hi = lax.reduce_precision(values, exponent_bits=8, mantissa_bits=7)
    rest = values - hi
    mid = lax.reduce_precision(rest, exponent_bits=8, mantissa_bits=7)
    return [hi, mid, rest - mid]


def body(
    tokens, expert_ids, router, w_gate, w_up, w_down, spike_level, queries, key_vectors, log_decay
):
    highest = lax.Precision.HIGHEST
    seq_axes = ("sz", "sy")
    count, width = tokens.shape
    n_experts = router.shape[1]
    heads = log_decay.shape[0]
    hd = queries.shape[1] // heads
    n_sz = lax.axis_size("sz")
    n_sy = lax.axis_size("sy")
    zi = lax.axis_index("sz")
    quarter = heads // n_sy
    qw = quarter * hd

    logits = jnp.dot(tokens, router, preferred_element_type=jnp.float32)
    matches = (
        expert_ids[:, :, None] == jnp.arange(n_experts, dtype=jnp.int32)[None, None, :]
    ).astype(jnp.float32)
    picked = jnp.sum(logits[:, None, :] * matches, axis=2)
    gate_first = jax.nn.sigmoid(picked[:, 0] - picked[:, 1])
    gate_second = jax.nn.sigmoid(picked[:, 1] - picked[:, 0])

    flat_ids = expert_ids.reshape(-1)
    entries = flat_ids.shape[0]
    one_hot = (flat_ids[:, None] == jnp.arange(n_experts, dtype=jnp.int32)[None, :]).astype(
        jnp.bfloat16
    )
    lower = (
        jnp.arange(entries)[:, None] >= jnp.arange(entries)[None, :]
    ).astype(jnp.bfloat16)
    running = jnp.dot(lower, one_hot, preferred_element_type=jnp.float32)
    slots = (jnp.sum(running * one_hot.astype(jnp.float32), axis=1) - 1.0).astype(jnp.int32)
    dest = flat_ids * SLOTS + slots
    n_rows = n_experts * SLOTS
    select = (jnp.arange(n_rows, dtype=jnp.int32)[:, None] == dest[None, :]).astype(jnp.bfloat16)
    select_tok = select.reshape(n_rows, count, 2).sum(axis=2)
    send = jnp.dot(select_tok, tokens, preferred_element_type=jnp.float32).astype(jnp.bfloat16)

    decay_parts = jnp.concatenate(split3(log_decay.reshape(n_sy, 1, quarter * count)), axis=1)
    slot_pairs = slots.reshape(count, 2).astype(jnp.float32)
    id_pairs = expert_ids.astype(jnp.float32)
    fields = [id_pairs[:, 0], slot_pairs[:, 0], id_pairs[:, 1], slot_pairs[:, 1]]
    fields += split3(gate_first) + split3(gate_second)
    n_fields = len(fields)
    info_rows = -(-(n_fields * count) // qw)
    info = jnp.stack(fields).reshape(-1)
    info = jnp.pad(info, (0, info_rows * qw - n_fields * count)).reshape(1, info_rows, qw)
    info = jnp.broadcast_to(info, (n_sy, info_rows, qw))
    q_split = queries.reshape(count, n_sy, qw).transpose(1, 0, 2)
    k_split = key_vectors.reshape(count, n_sy, qw).transpose(1, 0, 2)
    used = 2 * count + 3 + info_rows
    packed = jnp.concatenate(
        [
            q_split,
            k_split,
            decay_parts.astype(jnp.bfloat16),
            info.astype(jnp.bfloat16),
            jnp.zeros((n_sy, (-used) % 16, qw), jnp.bfloat16),
        ],
        axis=1,
    )
    got = lax.all_to_all(packed, "sy", 0, 0, tiled=True)
    group_q = got[:, :count].reshape(n_sy, count, quarter, hd)
    group_k = got[:, count : 2 * count].reshape(n_sy, count, quarter, hd)
    parts = got[:, 2 * count : 2 * count + 3].astype(jnp.float32)
    group_decay = (parts[:, 0] + parts[:, 1] + parts[:, 2]).reshape(n_sy, quarter, count)
    got_info = got[:, 2 * count + 3 : used].astype(jnp.float32).reshape(n_sy, info_rows * qw)
    got_info = got_info[:, : n_fields * count].reshape(n_sy, n_fields, count)
    g_first = (got_info[:, 4] + got_info[:, 5]) + got_info[:, 6]
    g_second = (got_info[:, 7] + got_info[:, 8]) + got_info[:, 9]
    row_first = (got_info[:, 0] * SLOTS + got_info[:, 1]).astype(jnp.int32)
    row_second = (got_info[:, 2] * SLOTS + got_info[:, 3]).astype(jnp.int32)

    recv = lax.all_to_all(send.reshape(n_experts, SLOTS, width), seq_axes, 0, 0, tiled=True)
    spikes = expert_spikes(recv.reshape(n_rows, width), w_gate[0], w_up[0], spike_level[0])
    outgoing = jnp.einsum(
        "zrk,kjc->zjrc",
        spikes.reshape(n_sz, n_sy * SLOTS, -1),
        w_down[0].reshape(-1, n_sy, qw),
        preferred_element_type=jnp.float32,
    ).astype(jnp.bfloat16)
    outgoing = outgoing.reshape(n_sz * n_sy, n_sy * SLOTS, qw)
    back = lax.all_to_all(outgoing, seq_axes, 0, 0, tiled=True)
    table = back.reshape(n_experts, n_sy, SLOTS, qw)
    lanes_e = jnp.arange(n_experts, dtype=jnp.int32)[None, None, :, None]
    lanes_s = jnp.arange(SLOTS, dtype=jnp.int32)[None, None, None, :]

    def pick(row):
        e = (row // SLOTS)[:, :, None, None]
        s = (row % SLOTS)[:, :, None, None]
        return ((e == lanes_e) & (s == lanes_s)).astype(jnp.bfloat16)

    first_out = jnp.einsum(
        "btes,ebsc->btc", pick(row_first), table, preferred_element_type=jnp.float32
    )
    second_out = jnp.einsum(
        "btes,ebsc->btc", pick(row_second), table, preferred_element_type=jnp.float32
    )
    mix_q = (g_first[:, :, None] * first_out + g_second[:, :, None] * second_out).astype(
        jnp.bfloat16
    )

    group_v = mix_q.reshape(n_sy, count, quarter, hd)
    cumulative = jnp.cumsum(group_decay, axis=2)
    scores = jnp.einsum(
        "bthd,bshd->bhts", group_q, group_k, preferred_element_type=jnp.float32
    )
    causal = jnp.arange(count)[:, None] >= jnp.arange(count)[None, :]
    spread = cumulative[:, :, :, None] - cumulative[:, :, None, :]
    decay = jnp.where(causal[None, None], jnp.exp(jnp.minimum(spread, 0.0)), 0.0)
    weights = (scores * decay).astype(jnp.bfloat16)
    intra = jnp.einsum("bhts,bshd->bthd", weights, group_v, preferred_element_type=jnp.float32)

    tail = jnp.exp(cumulative[:, :, -1:] - cumulative)
    scaled_k = group_k.astype(jnp.float32) * jnp.transpose(tail, (0, 2, 1))[:, :, :, None]
    local_states = jnp.einsum(
        "bshd,bshe->bhde", scaled_k, group_v.astype(jnp.float32), precision=highest
    )
    block_total = jnp.exp(cumulative[:, :, -1])

    run = jnp.zeros((quarter, hd, hd), jnp.float32)
    lead = jnp.ones((quarter,), jnp.float32)
    inside, leads = [], []
    for b in range(n_sy):
        inside.append(run)
        leads.append(lead)
        run = block_total[b][:, None, None] * run + local_states[b]
        lead = lead * block_total[b]
    group_state, group_span = run, lead

    state_rows = quarter * hd

    def pack(value, span):
        span_rows = jnp.zeros((8, hd), jnp.float32).at[0, :quarter].set(span)
        return jnp.concatenate([value.reshape(state_rows, hd), span_rows], axis=0)

    def unpack(packed):
        return packed[:state_rows].reshape(quarter, hd, hd), packed[state_rows, :quarter]

    def shifted(packed, by):
        pairs = [(i, i + by) for i in range(n_sz - by)]
        got_value, got_span = unpack(lax.ppermute(packed, "sz", pairs))
        return got_value, jnp.where(zi >= by, got_span, 1.0)

    def join(earlier, later):
        (v_e, s_e), (v_l, s_l) = earlier, later
        return (s_l[:, None, None] * v_e + v_l, s_e * s_l)

    own = pack(group_state, group_span)
    window = join(shifted(own, 2), shifted(own, 1))
    reach = 2
    while reach < n_sz:
        window = join(shifted(pack(*window), reach), window)
        reach *= 2
    before = window[0]

    carried = jnp.stack(leads)[:, :, None, None] * before[None] + jnp.stack(inside)
    inter = jnp.transpose(jnp.exp(cumulative), (0, 2, 1))[:, :, :, None] * jnp.einsum(
        "bthd,bhde->bthe", group_q.astype(jnp.float32), carried, precision=highest
    )
    total_out = intra + inter
    normed = total_out * lax.rsqrt(jnp.mean(total_out * total_out, axis=3, keepdims=True) + 1e-06)
    att_q = normed.astype(jnp.bfloat16).reshape(n_sy, count, qw)
    yi = lax.axis_index("sy")
    outgoing_home = jnp.stack([mix_q, att_q], axis=1)
    expert_mix = jnp.zeros((count, width), jnp.bfloat16)
    attended = jnp.zeros((count, heads * hd), jnp.bfloat16)
    for by in range(n_sy):
        piece = lax.dynamic_index_in_dim(outgoing_home, (yi + by) % n_sy, 0, False)
        if by:
            piece = lax.ppermute(piece, "sy", [(i, (i + by) % n_sy) for i in range(n_sy)])
        column = ((yi - by) % n_sy) * qw
        expert_mix = lax.dynamic_update_slice(expert_mix, piece[0], (0, column))
        attended = lax.dynamic_update_slice(attended, piece[1], (0, column))
    return (expert_mix, attended)


def solution(mesh):
    n_dp = mesh.shape["dp"]
    n_seq = mesh.shape["seq"]
    inner = Mesh(mesh.devices.reshape(n_dp, n_seq // GROUP, GROUP), ("dp", "sz", "sy"))
    rows = ("dp", "sz", "sy")
    in_specs = (
        P(rows, None),
        P(rows, None),
        P(),
        P(("sz", "sy"), None, None),
        P(("sz", "sy"), None, None),
        P(("sz", "sy"), None, None),
        P(("sz", "sy"), None),
        P(rows, None),
        P(rows, None),
        P(None, rows),
    )
    out_specs = (P(rows, None), P(rows, None))
    return jax.shard_map(body, mesh=inner, in_specs=in_specs, out_specs=out_specs, check_vma=False)
```

```python
import jax
import jax.numpy as jnp
from jax import lax
from jax.sharding import Mesh
from jax.sharding import PartitionSpec as P

SLOTS = 16
GROUP = 4


def expert_spikes(token_rows, gate_matrix, up_matrix, levels):
    gate_values = jnp.dot(token_rows, gate_matrix, preferred_element_type=jnp.float32)
    up_values = jnp.dot(token_rows, up_matrix, preferred_element_type=jnp.float32)
    hidden = jax.nn.silu(gate_values) * up_values
    threshold = 0.125 * levels.astype(jnp.float32)
    return (threshold * jnp.tanh(hidden / threshold)).astype(jnp.bfloat16)


def split3(values):
    hi = lax.reduce_precision(values, exponent_bits=8, mantissa_bits=7)
    rest = values - hi
    mid = lax.reduce_precision(rest, exponent_bits=8, mantissa_bits=7)
    return [hi, mid, rest - mid]


def body(
    tokens, expert_ids, router, w_gate, w_up, w_down, spike_level, queries, key_vectors, log_decay
):
    highest = lax.Precision.HIGHEST
    seq_axes = ("sz", "sy")
    count, width = tokens.shape
    n_experts = router.shape[1]
    heads = log_decay.shape[0]
    hd = queries.shape[1] // heads
    n_sz = lax.axis_size("sz")
    n_sy = lax.axis_size("sy")
    zi = lax.axis_index("sz")
    quarter = heads // n_sy
    qw = quarter * hd

    logits = jnp.dot(tokens, router, preferred_element_type=jnp.float32)
    matches = (
        expert_ids[:, :, None] == jnp.arange(n_experts, dtype=jnp.int32)[None, None, :]
    ).astype(jnp.float32)
    picked = jnp.sum(logits[:, None, :] * matches, axis=2)
    gate_first = jax.nn.sigmoid(picked[:, 0] - picked[:, 1])
    gate_second = jax.nn.sigmoid(picked[:, 1] - picked[:, 0])

    flat_ids = expert_ids.reshape(-1)
    entries = flat_ids.shape[0]
    one_hot = (flat_ids[:, None] == jnp.arange(n_experts, dtype=jnp.int32)[None, :]).astype(
        jnp.bfloat16
    )
    lower = (
        jnp.arange(entries)[:, None] >= jnp.arange(entries)[None, :]
    ).astype(jnp.bfloat16)
    running = jnp.dot(lower, one_hot, preferred_element_type=jnp.float32)
    slots = (jnp.sum(running * one_hot.astype(jnp.float32), axis=1) - 1.0).astype(jnp.int32)
    dest = flat_ids * SLOTS + slots
    n_rows = n_experts * SLOTS
    select = (jnp.arange(n_rows, dtype=jnp.int32)[:, None] == dest[None, :]).astype(jnp.bfloat16)
    select_tok = select.reshape(n_rows, count, 2).sum(axis=2)
    send = jnp.dot(select_tok, tokens, preferred_element_type=jnp.float32).astype(jnp.bfloat16)

    decay_parts = jnp.concatenate(split3(log_decay.reshape(n_sy, 1, quarter * count)), axis=1)
    slot_pairs = slots.reshape(count, 2).astype(jnp.float32)
    id_pairs = expert_ids.astype(jnp.float32)
    fields = [id_pairs[:, 0], slot_pairs[:, 0], id_pairs[:, 1], slot_pairs[:, 1]]
    fields += split3(gate_first) + split3(gate_second)
    n_fields = len(fields)
    info_rows = -(-(n_fields * count) // qw)
    info = jnp.stack(fields).reshape(-1)
    info = jnp.pad(info, (0, info_rows * qw - n_fields * count)).reshape(1, info_rows, qw)
    info = jnp.broadcast_to(info, (n_sy, info_rows, qw))
    q_split = queries.reshape(count, n_sy, qw).transpose(1, 0, 2)
    k_split = key_vectors.reshape(count, n_sy, qw).transpose(1, 0, 2)
    used = 2 * count + 3 + info_rows
    packed = jnp.concatenate(
        [
            q_split,
            k_split,
            decay_parts.astype(jnp.bfloat16),
            info.astype(jnp.bfloat16),
            jnp.zeros((n_sy, (-used) % 16, qw), jnp.bfloat16),
        ],
        axis=1,
    )
    got = lax.all_to_all(packed, "sy", 0, 0, tiled=True)
    group_q = got[:, :count].reshape(n_sy, count, quarter, hd)
    group_k = got[:, count : 2 * count].reshape(n_sy, count, quarter, hd)
    parts = got[:, 2 * count : 2 * count + 3].astype(jnp.float32)
    group_decay = (parts[:, 0] + parts[:, 1] + parts[:, 2]).reshape(n_sy, quarter, count)
    got_info = got[:, 2 * count + 3 : used].astype(jnp.float32).reshape(n_sy, info_rows * qw)
    got_info = got_info[:, : n_fields * count].reshape(n_sy, n_fields, count)
    g_first = (got_info[:, 4] + got_info[:, 5]) + got_info[:, 6]
    g_second = (got_info[:, 7] + got_info[:, 8]) + got_info[:, 9]
    row_first = (got_info[:, 0] * SLOTS + got_info[:, 1]).astype(jnp.int32)
    row_second = (got_info[:, 2] * SLOTS + got_info[:, 3]).astype(jnp.int32)

    recv = lax.all_to_all(send.reshape(n_experts, SLOTS, width), seq_axes, 0, 0, tiled=True)
    spikes = expert_spikes(recv.reshape(n_rows, width), w_gate[0], w_up[0], spike_level[0])
    outgoing = jnp.einsum(
        "zrk,kjc->zjrc",
        spikes.reshape(n_sz, n_sy * SLOTS, -1),
        w_down[0].reshape(-1, n_sy, qw),
        preferred_element_type=jnp.float32,
    ).astype(jnp.bfloat16)
    outgoing = outgoing.reshape(n_sz * n_sy, n_sy * SLOTS, qw)
    back = lax.all_to_all(outgoing, seq_axes, 0, 0, tiled=True)
    table = back.reshape(n_experts, n_sy, SLOTS, qw)
    lanes_e = jnp.arange(n_experts, dtype=jnp.int32)[None, None, :, None]
    lanes_s = jnp.arange(SLOTS, dtype=jnp.int32)[None, None, None, :]

    def pick(row):
        e = (row // SLOTS)[:, :, None, None]
        s = (row % SLOTS)[:, :, None, None]
        return ((e == lanes_e) & (s == lanes_s)).astype(jnp.bfloat16)

    first_out = jnp.einsum(
        "btes,ebsc->btc", pick(row_first), table, preferred_element_type=jnp.float32
    )
    second_out = jnp.einsum(
        "btes,ebsc->btc", pick(row_second), table, preferred_element_type=jnp.float32
    )
    mix_q = (g_first[:, :, None] * first_out + g_second[:, :, None] * second_out).astype(
        jnp.bfloat16
    )

    group_v = mix_q.reshape(n_sy, count, quarter, hd)
    cumulative = jnp.cumsum(group_decay, axis=2)
    scores = jnp.einsum(
        "bthd,bshd->bhts", group_q, group_k, preferred_element_type=jnp.float32
    )
    causal = jnp.arange(count)[:, None] >= jnp.arange(count)[None, :]
    spread = cumulative[:, :, :, None] - cumulative[:, :, None, :]
    decay = jnp.where(causal[None, None], jnp.exp(jnp.minimum(spread, 0.0)), 0.0)
    weights = (scores * decay).astype(jnp.bfloat16)
    intra = jnp.einsum("bhts,bshd->bthd", weights, group_v, preferred_element_type=jnp.float32)

    tail = jnp.exp(cumulative[:, :, -1:] - cumulative)
    scaled_k = group_k.astype(jnp.float32) * jnp.transpose(tail, (0, 2, 1))[:, :, :, None]
    local_states = jnp.einsum(
        "bshd,bshe->bhde", scaled_k, group_v.astype(jnp.float32), precision=highest
    )
    block_total = jnp.exp(cumulative[:, :, -1])

    run = jnp.zeros((quarter, hd, hd), jnp.float32)
    lead = jnp.ones((quarter,), jnp.float32)
    inside, leads = [], []
    for b in range(n_sy):
        inside.append(run)
        leads.append(lead)
        run = block_total[b][:, None, None] * run + local_states[b]
        lead = lead * block_total[b]
    group_state, group_span = run, lead

    growth = jnp.transpose(jnp.exp(cumulative), (0, 2, 1))[:, :, :, None]
    q32 = group_q.astype(jnp.float32)
    near = intra + growth * jnp.einsum(
        "bthd,bhde->bthe", q32, jnp.stack(inside), precision=highest
    )

    yi = lax.axis_index("sy")

    def send_home(quarters, total_width):
        assembled = jnp.zeros((count, total_width), jnp.bfloat16)
        for by in range(n_sy):
            piece = lax.dynamic_index_in_dim(quarters, (yi + by) % n_sy, 0, False)
            if by:
                piece = lax.ppermute(piece, "sy", [(i, (i + by) % n_sy) for i in range(n_sy)])
            assembled = lax.dynamic_update_slice(assembled, piece, (0, ((yi - by) % n_sy) * qw))
        return assembled

    expert_mix = send_home(mix_q, width)

    state_rows = quarter * hd

    def pack(value, span):
        span_rows = jnp.zeros((8, hd), jnp.float32).at[0, :quarter].set(span)
        return jnp.concatenate([value.reshape(state_rows, hd), span_rows], axis=0)

    def unpack(packed):
        return packed[:state_rows].reshape(quarter, hd, hd), packed[state_rows, :quarter]

    def shifted(packed, by):
        pairs = [(i, i + by) for i in range(n_sz - by)]
        got_value, got_span = unpack(lax.ppermute(packed, "sz", pairs))
        return got_value, jnp.where(zi >= by, got_span, 1.0)

    def join(earlier, later):
        (v_e, s_e), (v_l, s_l) = earlier, later
        return (s_l[:, None, None] * v_e + v_l, s_e * s_l)

    own = pack(group_state, group_span)
    window = join(shifted(own, 2), shifted(own, 1))
    reach = 2
    while reach < n_sz:
        window = join(shifted(pack(*window), reach), window)
        reach *= 2
    before = window[0]

    far = jnp.stack(leads)[:, :, None, None] * before[None]
    total_out = near + growth * jnp.einsum("bthd,bhde->bthe", q32, far, precision=highest)
    normed = total_out * lax.rsqrt(jnp.mean(total_out * total_out, axis=3, keepdims=True) + 1e-06)
    att_q = normed.astype(jnp.bfloat16).reshape(n_sy, count, qw)
    attended = send_home(att_q, heads * hd)
    return (expert_mix, attended)


def solution(mesh):
    n_dp = mesh.shape["dp"]
    n_seq = mesh.shape["seq"]
    inner = Mesh(mesh.devices.reshape(n_dp, n_seq // GROUP, GROUP), ("dp", "sz", "sy"))
    rows = ("dp", "sz", "sy")
    in_specs = (
        P(rows, None),
        P(rows, None),
        P(),
        P(("sz", "sy"), None, None),
        P(("sz", "sy"), None, None),
        P(("sz", "sy"), None, None),
        P(("sz", "sy"), None),
        P(rows, None),
        P(rows, None),
        P(None, rows),
    )
    out_specs = (P(rows, None), P(rows, None))
    return jax.shard_map(body, mesh=inner, in_specs=in_specs, out_specs=out_specs, check_vma=False)
```

```python
import jax
import jax.numpy as jnp
from jax import lax
from jax.sharding import Mesh
from jax.sharding import PartitionSpec as P

SLOTS = 16
GROUP = 4


def expert_spikes(token_rows, gate_matrix, up_matrix, levels):
    gate_values = jnp.dot(token_rows, gate_matrix, preferred_element_type=jnp.float32)
    up_values = jnp.dot(token_rows, up_matrix, preferred_element_type=jnp.float32)
    hidden = jax.nn.silu(gate_values) * up_values
    threshold = 0.125 * levels.astype(jnp.float32)
    return (threshold * jnp.tanh(hidden / threshold)).astype(jnp.bfloat16)


def split3(values):
    hi = lax.reduce_precision(values, exponent_bits=8, mantissa_bits=7)
    rest = values - hi
    mid = lax.reduce_precision(rest, exponent_bits=8, mantissa_bits=7)
    return [hi, mid, rest - mid]


def body(
    tokens, expert_ids, router, w_gate, w_up, w_down, spike_level, queries, key_vectors, log_decay
):
    highest = lax.Precision.HIGHEST
    seq_axes = ("sz", "sy")
    count, width = tokens.shape
    n_experts = router.shape[1]
    heads = log_decay.shape[0]
    hd = queries.shape[1] // heads
    n_sz = lax.axis_size("sz")
    n_sy = lax.axis_size("sy")
    zi = lax.axis_index("sz")
    quarter = heads // n_sy
    qw = quarter * hd

    logits = jnp.dot(tokens, router, preferred_element_type=jnp.float32)
    matches = (
        expert_ids[:, :, None] == jnp.arange(n_experts, dtype=jnp.int32)[None, None, :]
    ).astype(jnp.float32)
    picked = jnp.sum(logits[:, None, :] * matches, axis=2)
    gate_first = jax.nn.sigmoid(picked[:, 0] - picked[:, 1])
    gate_second = jax.nn.sigmoid(picked[:, 1] - picked[:, 0])

    flat_ids = expert_ids.reshape(-1)
    entries = flat_ids.shape[0]
    one_hot = (flat_ids[:, None] == jnp.arange(n_experts, dtype=jnp.int32)[None, :]).astype(
        jnp.bfloat16
    )
    lower = (
        jnp.arange(entries)[:, None] >= jnp.arange(entries)[None, :]
    ).astype(jnp.bfloat16)
    running = jnp.dot(lower, one_hot, preferred_element_type=jnp.float32)
    slots = (jnp.sum(running * one_hot.astype(jnp.float32), axis=1) - 1.0).astype(jnp.int32)
    dest = flat_ids * SLOTS + slots
    n_rows = n_experts * SLOTS
    select = (jnp.arange(n_rows, dtype=jnp.int32)[:, None] == dest[None, :]).astype(jnp.bfloat16)
    select_tok = select.reshape(n_rows, count, 2).sum(axis=2)
    send = jnp.dot(select_tok, tokens, preferred_element_type=jnp.float32).astype(jnp.bfloat16)

    decay_parts = jnp.concatenate(split3(log_decay.reshape(n_sy, 1, quarter * count)), axis=1)
    slot_pairs = slots.reshape(count, 2).astype(jnp.float32)
    id_pairs = expert_ids.astype(jnp.float32)
    fields = [id_pairs[:, 0], slot_pairs[:, 0], id_pairs[:, 1], slot_pairs[:, 1]]
    fields += split3(gate_first) + split3(gate_second)
    n_fields = len(fields)
    info_rows = -(-(n_fields * count) // qw)
    info = jnp.stack(fields).reshape(-1)
    info = jnp.pad(info, (0, info_rows * qw - n_fields * count)).reshape(1, info_rows, qw)
    info = jnp.broadcast_to(info, (n_sy, info_rows, qw))
    q_split = queries.reshape(count, n_sy, qw).transpose(1, 0, 2)
    k_split = key_vectors.reshape(count, n_sy, qw).transpose(1, 0, 2)
    used = 2 * count + 3 + info_rows
    packed = jnp.concatenate(
        [
            q_split,
            k_split,
            decay_parts.astype(jnp.bfloat16),
            info.astype(jnp.bfloat16),
            jnp.zeros((n_sy, (-used) % 16, qw), jnp.bfloat16),
        ],
        axis=1,
    )
    yi = lax.axis_index("sy")
    got = jnp.zeros_like(packed)
    for by in range(n_sy):
        piece = lax.dynamic_index_in_dim(packed, (yi + by) % n_sy, 0, True)
        if by:
            piece = lax.ppermute(piece, "sy", [(i, (i + by) % n_sy) for i in range(n_sy)])
        got = lax.dynamic_update_slice(got, piece, ((yi - by) % n_sy, 0, 0))
    recv = lax.all_to_all(send.reshape(n_experts, SLOTS, width), seq_axes, 0, 0, tiled=True)
    spikes = expert_spikes(recv.reshape(n_rows, width), w_gate[0], w_up[0], spike_level[0])
    group_q = got[:, :count].reshape(n_sy, count, quarter, hd)
    group_k = got[:, count : 2 * count].reshape(n_sy, count, quarter, hd)
    parts = got[:, 2 * count : 2 * count + 3].astype(jnp.float32)
    group_decay = (parts[:, 0] + parts[:, 1] + parts[:, 2]).reshape(n_sy, quarter, count)
    got_info = got[:, 2 * count + 3 : used].astype(jnp.float32).reshape(n_sy, info_rows * qw)
    got_info = got_info[:, : n_fields * count].reshape(n_sy, n_fields, count)
    g_first = (got_info[:, 4] + got_info[:, 5]) + got_info[:, 6]
    g_second = (got_info[:, 7] + got_info[:, 8]) + got_info[:, 9]
    row_first = (got_info[:, 0] * SLOTS + got_info[:, 1]).astype(jnp.int32)
    row_second = (got_info[:, 2] * SLOTS + got_info[:, 3]).astype(jnp.int32)

    outgoing = jnp.einsum(
        "zrk,kjc->zjrc",
        spikes.reshape(n_sz, n_sy * SLOTS, -1),
        w_down[0].reshape(-1, n_sy, qw),
        preferred_element_type=jnp.float32,
    ).astype(jnp.bfloat16)
    outgoing = outgoing.reshape(n_sz * n_sy, n_sy * SLOTS, qw)
    back = lax.all_to_all(outgoing, seq_axes, 0, 0, tiled=True)
    table = back.reshape(n_experts, n_sy, SLOTS, qw)
    lanes_e = jnp.arange(n_experts, dtype=jnp.int32)[None, None, :, None]
    lanes_s = jnp.arange(SLOTS, dtype=jnp.int32)[None, None, None, :]

    def pick(row):
        e = (row // SLOTS)[:, :, None, None]
        s = (row % SLOTS)[:, :, None, None]
        return ((e == lanes_e) & (s == lanes_s)).astype(jnp.bfloat16)

    first_out = jnp.einsum(
        "btes,ebsc->btc", pick(row_first), table, preferred_element_type=jnp.float32
    )
    second_out = jnp.einsum(
        "btes,ebsc->btc", pick(row_second), table, preferred_element_type=jnp.float32
    )
    mix_q = (g_first[:, :, None] * first_out + g_second[:, :, None] * second_out).astype(
        jnp.bfloat16
    )

    group_v = mix_q.reshape(n_sy, count, quarter, hd)
    cumulative = jnp.cumsum(group_decay, axis=2)
    scores = jnp.einsum(
        "bthd,bshd->bhts", group_q, group_k, preferred_element_type=jnp.float32
    )
    causal = jnp.arange(count)[:, None] >= jnp.arange(count)[None, :]
    spread = cumulative[:, :, :, None] - cumulative[:, :, None, :]
    decay = jnp.where(causal[None, None], jnp.exp(jnp.minimum(spread, 0.0)), 0.0)
    weights = (scores * decay).astype(jnp.bfloat16)
    intra = jnp.einsum("bhts,bshd->bthd", weights, group_v, preferred_element_type=jnp.float32)

    tail = jnp.exp(cumulative[:, :, -1:] - cumulative)
    scaled_k = group_k.astype(jnp.float32) * jnp.transpose(tail, (0, 2, 1))[:, :, :, None]
    local_states = jnp.einsum(
        "bshd,bshe->bhde", scaled_k, group_v.astype(jnp.float32), precision=highest
    )
    block_total = jnp.exp(cumulative[:, :, -1])

    run = jnp.zeros((quarter, hd, hd), jnp.float32)
    lead = jnp.ones((quarter,), jnp.float32)
    inside, leads = [], []
    for b in range(n_sy):
        inside.append(run)
        leads.append(lead)
        run = block_total[b][:, None, None] * run + local_states[b]
        lead = lead * block_total[b]
    group_state, group_span = run, lead

    growth = jnp.transpose(jnp.exp(cumulative), (0, 2, 1))[:, :, :, None]
    q32 = group_q.astype(jnp.float32)
    near = intra + growth * jnp.einsum(
        "bthd,bhde->bthe", q32, jnp.stack(inside), precision=highest
    )


    def send_home(quarters, total_width):
        assembled = jnp.zeros((count, total_width), jnp.bfloat16)
        for by in range(n_sy):
            piece = lax.dynamic_index_in_dim(quarters, (yi + by) % n_sy, 0, False)
            if by:
                piece = lax.ppermute(piece, "sy", [(i, (i + by) % n_sy) for i in range(n_sy)])
            assembled = lax.dynamic_update_slice(assembled, piece, (0, ((yi - by) % n_sy) * qw))
        return assembled

    expert_mix = send_home(mix_q, width)

    state_rows = quarter * hd

    def pack(value, span):
        span_rows = jnp.zeros((8, hd), jnp.float32).at[0, :quarter].set(span)
        return jnp.concatenate([value.reshape(state_rows, hd), span_rows], axis=0)

    def unpack(packed):
        return packed[:state_rows].reshape(quarter, hd, hd), packed[state_rows, :quarter]

    def shifted(packed, by):
        pairs = [(i, i + by) for i in range(n_sz - by)]
        got_value, got_span = unpack(lax.ppermute(packed, "sz", pairs))
        return got_value, jnp.where(zi >= by, got_span, 1.0)

    def join(earlier, later):
        (v_e, s_e), (v_l, s_l) = earlier, later
        return (s_l[:, None, None] * v_e + v_l, s_e * s_l)

    own = pack(group_state, group_span)
    window = join(shifted(own, 2), shifted(own, 1))
    reach = 2
    while reach < n_sz:
        window = join(shifted(pack(*window), reach), window)
        reach *= 2
    before = window[0]

    far = jnp.stack(leads)[:, :, None, None] * before[None]
    total_out = near + growth * jnp.einsum("bthd,bhde->bthe", q32, far, precision=highest)
    normed = total_out * lax.rsqrt(jnp.mean(total_out * total_out, axis=3, keepdims=True) + 1e-06)
    att_q = normed.astype(jnp.bfloat16).reshape(n_sy, count, qw)
    attended = send_home(att_q, heads * hd)
    return (expert_mix, attended)


def solution(mesh):
    n_dp = mesh.shape["dp"]
    n_seq = mesh.shape["seq"]
    inner = Mesh(mesh.devices.reshape(n_dp, n_seq // GROUP, GROUP), ("dp", "sz", "sy"))
    rows = ("dp", "sz", "sy")
    in_specs = (
        P(rows, None),
        P(rows, None),
        P(),
        P(("sz", "sy"), None, None),
        P(("sz", "sy"), None, None),
        P(("sz", "sy"), None, None),
        P(("sz", "sy"), None),
        P(rows, None),
        P(rows, None),
        P(None, rows),
    )
    out_specs = (P(rows, None), P(rows, None))
    return jax.shard_map(body, mesh=inner, in_specs=in_specs, out_specs=out_specs, check_vma=False)
```

```python
import jax
import jax.numpy as jnp
from jax import lax
from jax.sharding import Mesh
from jax.sharding import PartitionSpec as P

SLOTS = 16
GROUP = 4


def expert_spikes(token_rows, gate_matrix, up_matrix, levels):
    gate_values = jnp.dot(token_rows, gate_matrix, preferred_element_type=jnp.float32)
    up_values = jnp.dot(token_rows, up_matrix, preferred_element_type=jnp.float32)
    hidden = jax.nn.silu(gate_values) * up_values
    threshold = 0.125 * levels.astype(jnp.float32)
    return (threshold * jnp.tanh(hidden / threshold)).astype(jnp.bfloat16)


def split3(values):
    hi = lax.reduce_precision(values, exponent_bits=8, mantissa_bits=7)
    rest = values - hi
    mid = lax.reduce_precision(rest, exponent_bits=8, mantissa_bits=7)
    return [hi, mid, rest - mid]


def body(
    tokens, expert_ids, router, w_gate, w_up, w_down, spike_level, queries, key_vectors, log_decay
):
    highest = lax.Precision.HIGHEST
    seq_axes = ("sz", "sy")
    count, width = tokens.shape
    n_experts = router.shape[1]
    heads = log_decay.shape[0]
    hd = queries.shape[1] // heads
    n_sz = lax.axis_size("sz")
    n_sy = lax.axis_size("sy")
    zi = lax.axis_index("sz")
    quarter = heads // n_sy
    qw = quarter * hd

    logits = jnp.dot(tokens, router, preferred_element_type=jnp.float32)
    matches = (
        expert_ids[:, :, None] == jnp.arange(n_experts, dtype=jnp.int32)[None, None, :]
    ).astype(jnp.float32)
    picked = jnp.sum(logits[:, None, :] * matches, axis=2)
    gate_first = jax.nn.sigmoid(picked[:, 0] - picked[:, 1])
    gate_second = jax.nn.sigmoid(picked[:, 1] - picked[:, 0])

    flat_ids = expert_ids.reshape(-1)
    entries = flat_ids.shape[0]
    one_hot = (flat_ids[:, None] == jnp.arange(n_experts, dtype=jnp.int32)[None, :]).astype(
        jnp.bfloat16
    )
    lower = (
        jnp.arange(entries)[:, None] >= jnp.arange(entries)[None, :]
    ).astype(jnp.bfloat16)
    running = jnp.dot(lower, one_hot, preferred_element_type=jnp.float32)
    slots = (jnp.sum(running * one_hot.astype(jnp.float32), axis=1) - 1.0).astype(jnp.int32)
    dest = flat_ids * SLOTS + slots
    n_rows = n_experts * SLOTS
    select = (jnp.arange(n_rows, dtype=jnp.int32)[:, None] == dest[None, :]).astype(jnp.bfloat16)
    select_tok = select.reshape(n_rows, count, 2).sum(axis=2)
    send = jnp.dot(select_tok, tokens, preferred_element_type=jnp.float32).astype(jnp.bfloat16)

    decay_parts = jnp.concatenate(split3(log_decay.reshape(n_sy, 1, quarter * count)), axis=1)
    slot_pairs = slots.reshape(count, 2).astype(jnp.float32)
    id_pairs = expert_ids.astype(jnp.float32)
    fields = [id_pairs[:, 0], slot_pairs[:, 0], id_pairs[:, 1], slot_pairs[:, 1]]
    fields += split3(gate_first) + split3(gate_second)
    n_fields = len(fields)
    info_rows = -(-(n_fields * count) // qw)
    info = jnp.stack(fields).reshape(-1)
    info = jnp.pad(info, (0, info_rows * qw - n_fields * count)).reshape(1, info_rows, qw)
    info = jnp.broadcast_to(info, (n_sy, info_rows, qw))
    q_split = queries.reshape(count, n_sy, qw).transpose(1, 0, 2)
    k_split = key_vectors.reshape(count, n_sy, qw).transpose(1, 0, 2)
    used = 2 * count + 3 + info_rows
    packed = jnp.concatenate(
        [
            q_split,
            k_split,
            decay_parts.astype(jnp.bfloat16),
            info.astype(jnp.bfloat16),
            jnp.zeros((n_sy, (-used) % 16, qw), jnp.bfloat16),
        ],
        axis=1,
    )
    yi = lax.axis_index("sy")
    got = jnp.zeros_like(packed)
    for by in range(n_sy):
        piece = lax.dynamic_index_in_dim(packed, (yi + by) % n_sy, 0, True)
        if by:
            piece = lax.ppermute(piece, "sy", [(i, (i + by) % n_sy) for i in range(n_sy)])
        got = lax.dynamic_update_slice(got, piece, ((yi - by) % n_sy, 0, 0))
    recv = lax.all_to_all(send.reshape(n_experts, SLOTS, width), seq_axes, 0, 0, tiled=True)
    spikes = expert_spikes(recv.reshape(n_rows, width), w_gate[0], w_up[0], spike_level[0])
    group_q = got[:, :count].reshape(n_sy, count, quarter, hd)
    group_k = got[:, count : 2 * count].reshape(n_sy, count, quarter, hd)
    parts = got[:, 2 * count : 2 * count + 3].astype(jnp.float32)
    group_decay = (parts[:, 0] + parts[:, 1] + parts[:, 2]).reshape(n_sy, quarter, count)
    got_info = got[:, 2 * count + 3 : used].astype(jnp.float32).reshape(n_sy, info_rows * qw)
    got_info = got_info[:, : n_fields * count].reshape(n_sy, n_fields, count)
    g_first = (got_info[:, 4] + got_info[:, 5]) + got_info[:, 6]
    g_second = (got_info[:, 7] + got_info[:, 8]) + got_info[:, 9]
    row_first = (got_info[:, 0] * SLOTS + got_info[:, 1]).astype(jnp.int32)
    row_second = (got_info[:, 2] * SLOTS + got_info[:, 3]).astype(jnp.int32)

    outgoing = jnp.einsum(
        "zrk,kjc->zjrc",
        spikes.reshape(n_sz, n_sy * SLOTS, -1),
        w_down[0].reshape(-1, n_sy, qw),
        preferred_element_type=jnp.float32,
    ).astype(jnp.bfloat16)
    outgoing = outgoing.reshape(n_sz * n_sy, n_sy * SLOTS, qw)
    back = lax.all_to_all(outgoing, seq_axes, 0, 0, tiled=True)
    table = back.reshape(n_experts, n_sy, SLOTS, qw)
    lanes_e = jnp.arange(n_experts, dtype=jnp.int32)[None, None, :, None]
    lanes_s = jnp.arange(SLOTS, dtype=jnp.int32)[None, None, None, :]

    def pick(row):
        e = (row // SLOTS)[:, :, None, None]
        s = (row % SLOTS)[:, :, None, None]
        return ((e == lanes_e) & (s == lanes_s)).astype(jnp.bfloat16)

    first_out = jnp.einsum(
        "btes,ebsc->btc", pick(row_first), table, preferred_element_type=jnp.float32
    )
    second_out = jnp.einsum(
        "btes,ebsc->btc", pick(row_second), table, preferred_element_type=jnp.float32
    )
    mix_q = (g_first[:, :, None] * first_out + g_second[:, :, None] * second_out).astype(
        jnp.bfloat16
    )

    group_v = mix_q.reshape(n_sy, count, quarter, hd)
    cumulative = jnp.cumsum(group_decay, axis=2)
    scores = jnp.einsum(
        "bthd,bshd->bhts", group_q, group_k, preferred_element_type=jnp.float32
    )
    causal = jnp.arange(count)[:, None] >= jnp.arange(count)[None, :]
    spread = cumulative[:, :, :, None] - cumulative[:, :, None, :]
    decay = jnp.where(causal[None, None], jnp.exp(jnp.minimum(spread, 0.0)), 0.0)
    weights = (scores * decay).astype(jnp.bfloat16)
    intra = jnp.einsum("bhts,bshd->bthd", weights, group_v, preferred_element_type=jnp.float32)

    tail = jnp.exp(cumulative[:, :, -1:] - cumulative)
    scaled_k = group_k.astype(jnp.float32) * jnp.transpose(tail, (0, 2, 1))[:, :, :, None]
    local_states = jnp.einsum(
        "bshd,bshe->bhde", scaled_k, group_v.astype(jnp.float32), precision=highest
    )
    block_total = jnp.exp(cumulative[:, :, -1])

    run = jnp.zeros((quarter, hd, hd), jnp.float32)
    lead = jnp.ones((quarter,), jnp.float32)
    inside, leads = [], []
    for b in range(n_sy):
        inside.append(run)
        leads.append(lead)
        run = block_total[b][:, None, None] * run + local_states[b]
        lead = lead * block_total[b]
    group_state, group_span = run, lead

    growth = jnp.transpose(jnp.exp(cumulative), (0, 2, 1))[:, :, :, None]
    q32 = group_q.astype(jnp.float32)
    near = intra + growth * jnp.einsum(
        "bthd,bhde->bthe", q32, jnp.stack(inside), precision=highest
    )


    def send_home(quarters, total_width):
        assembled = jnp.zeros((count, total_width), jnp.bfloat16)
        for by in range(n_sy):
            piece = lax.dynamic_index_in_dim(quarters, (yi + by) % n_sy, 0, False)
            if by:
                piece = lax.ppermute(piece, "sy", [(i, (i + by) % n_sy) for i in range(n_sy)])
            assembled = lax.dynamic_update_slice(assembled, piece, (0, ((yi - by) % n_sy) * qw))
        return assembled

    expert_mix = send_home(mix_q, width)

    state_rows = quarter * hd

    def pack(value, span):
        span_rows = jnp.zeros((8, hd), jnp.float32).at[0, :quarter].set(span)
        return jnp.concatenate([value.reshape(state_rows, hd), span_rows], axis=0)

    def unpack(packed):
        return packed[:state_rows].reshape(quarter, hd, hd), packed[state_rows, :quarter]

    def shifted(packed, by, first=0):
        pairs = [(i, i + by) for i in range(first, n_sz - by)]
        got_value, got_span = unpack(lax.ppermute(packed, "sz", pairs))
        return got_value, jnp.where(zi >= by, got_span, 1.0)

    def join(earlier, later):
        (v_e, s_e), (v_l, s_l) = earlier, later
        return (s_l[:, None, None] * v_e + v_l, s_e * s_l)

    own = pack(group_state, group_span)
    window = join(shifted(own, 2), shifted(own, 1))
    reach = 2
    while reach < n_sz:
        window = join(shifted(pack(*window), reach, first=1), window)
        reach *= 2
    before = window[0]

    far = jnp.stack(leads)[:, :, None, None] * before[None]
    total_out = near + growth * jnp.einsum("bthd,bhde->bthe", q32, far, precision=highest)
    normed = total_out * lax.rsqrt(jnp.mean(total_out * total_out, axis=3, keepdims=True) + 1e-06)
    att_q = normed.astype(jnp.bfloat16).reshape(n_sy, count, qw)
    attended = send_home(att_q, heads * hd)
    return (expert_mix, attended)


def solution(mesh):
    n_dp = mesh.shape["dp"]
    n_seq = mesh.shape["seq"]
    inner = Mesh(mesh.devices.reshape(n_dp, n_seq // GROUP, GROUP), ("dp", "sz", "sy"))
    rows = ("dp", "sz", "sy")
    in_specs = (
        P(rows, None),
        P(rows, None),
        P(),
        P(("sz", "sy"), None, None),
        P(("sz", "sy"), None, None),
        P(("sz", "sy"), None, None),
        P(("sz", "sy"), None),
        P(rows, None),
        P(rows, None),
        P(None, rows),
    )
    out_specs = (P(rows, None), P(rows, None))
    return jax.shard_map(body, mesh=inner, in_specs=in_specs, out_specs=out_specs, check_vma=False)
```

```python
import jax
import jax.numpy as jnp
from jax import lax
from jax.sharding import Mesh
from jax.sharding import PartitionSpec as P

SLOTS = 16
GROUP = 4


def expert_spikes(token_rows, gate_matrix, up_matrix, levels):
    gate_values = jnp.dot(token_rows, gate_matrix, preferred_element_type=jnp.float32)
    up_values = jnp.dot(token_rows, up_matrix, preferred_element_type=jnp.float32)
    hidden = jax.nn.silu(gate_values) * up_values
    threshold = 0.125 * levels.astype(jnp.float32)
    return (threshold * jnp.tanh(hidden / threshold)).astype(jnp.bfloat16)


def split3(values):
    hi = lax.reduce_precision(values, exponent_bits=8, mantissa_bits=7)
    rest = values - hi
    mid = lax.reduce_precision(rest, exponent_bits=8, mantissa_bits=7)
    return [hi, mid, rest - mid]


def body(
    tokens, expert_ids, router, w_gate, w_up, w_down, spike_level, queries, key_vectors, log_decay
):
    highest = lax.Precision.HIGHEST
    seq_axes = ("sz", "sy")
    count, width = tokens.shape
    n_experts = router.shape[1]
    heads = log_decay.shape[0]
    hd = queries.shape[1] // heads
    n_sz = lax.axis_size("sz")
    n_sy = lax.axis_size("sy")
    zi = lax.axis_index("sz")
    quarter = heads // n_sy
    qw = quarter * hd

    logits = jnp.dot(tokens, router, preferred_element_type=jnp.float32)
    matches = (
        expert_ids[:, :, None] == jnp.arange(n_experts, dtype=jnp.int32)[None, None, :]
    ).astype(jnp.float32)
    picked = jnp.sum(logits[:, None, :] * matches, axis=2)
    gate_first = jax.nn.sigmoid(picked[:, 0] - picked[:, 1])
    gate_second = jax.nn.sigmoid(picked[:, 1] - picked[:, 0])

    flat_ids = expert_ids.reshape(-1)
    entries = flat_ids.shape[0]
    one_hot = (flat_ids[:, None] == jnp.arange(n_experts, dtype=jnp.int32)[None, :]).astype(
        jnp.bfloat16
    )
    lower = (
        jnp.arange(entries)[:, None] >= jnp.arange(entries)[None, :]
    ).astype(jnp.bfloat16)
    running = jnp.dot(lower, one_hot, preferred_element_type=jnp.float32)
    slots = (jnp.sum(running * one_hot.astype(jnp.float32), axis=1) - 1.0).astype(jnp.int32)
    dest = flat_ids * SLOTS + slots
    n_rows = n_experts * SLOTS
    select = (jnp.arange(n_rows, dtype=jnp.int32)[:, None] == dest[None, :]).astype(jnp.bfloat16)
    select_tok = select.reshape(n_rows, count, 2).sum(axis=2)
    send = jnp.dot(select_tok, tokens, preferred_element_type=jnp.float32).astype(jnp.bfloat16)

    decay_parts = jnp.concatenate(split3(log_decay.reshape(n_sy, 1, quarter * count)), axis=1)
    slot_pairs = slots.reshape(count, 2).astype(jnp.float32)
    id_pairs = expert_ids.astype(jnp.float32)
    fields = [id_pairs[:, 0], slot_pairs[:, 0], id_pairs[:, 1], slot_pairs[:, 1]]
    fields += split3(gate_first) + split3(gate_second)
    n_fields = len(fields)
    info_rows = -(-(n_fields * count) // qw)
    info = jnp.stack(fields).reshape(-1)
    info = jnp.pad(info, (0, info_rows * qw - n_fields * count)).reshape(1, info_rows, qw)
    info = jnp.broadcast_to(info, (n_sy, info_rows, qw))
    q_split = queries.reshape(count, n_sy, qw).transpose(1, 0, 2)
    k_split = key_vectors.reshape(count, n_sy, qw).transpose(1, 0, 2)
    used = 2 * count + 3 + info_rows
    packed = jnp.concatenate(
        [
            q_split,
            k_split,
            decay_parts.astype(jnp.bfloat16),
            info.astype(jnp.bfloat16),
            jnp.zeros((n_sy, (-used) % 16, qw), jnp.bfloat16),
        ],
        axis=1,
    )
    yi = lax.axis_index("sy")
    got = jnp.zeros_like(packed)
    for by in range(n_sy):
        piece = lax.dynamic_index_in_dim(packed, (yi + by) % n_sy, 0, True)
        if by:
            piece = lax.ppermute(piece, "sy", [(i, (i + by) % n_sy) for i in range(n_sy)])
        got = lax.dynamic_update_slice(got, piece, ((yi - by) % n_sy, 0, 0))
    recv = lax.all_to_all(send.reshape(n_experts, SLOTS, width), seq_axes, 0, 0, tiled=True)
    spikes = expert_spikes(recv.reshape(n_rows, width), w_gate[0], w_up[0], spike_level[0])
    group_q = got[:, :count].reshape(n_sy, count, quarter, hd)
    group_k = got[:, count : 2 * count].reshape(n_sy, count, quarter, hd)
    parts = got[:, 2 * count : 2 * count + 3].astype(jnp.float32)
    group_decay = (parts[:, 0] + parts[:, 1] + parts[:, 2]).reshape(n_sy, quarter, count)
    got_info = got[:, 2 * count + 3 : used].astype(jnp.float32).reshape(n_sy, info_rows * qw)
    got_info = got_info[:, : n_fields * count].reshape(n_sy, n_fields, count)
    g_first = (got_info[:, 4] + got_info[:, 5]) + got_info[:, 6]
    g_second = (got_info[:, 7] + got_info[:, 8]) + got_info[:, 9]
    row_first = (got_info[:, 0] * SLOTS + got_info[:, 1]).astype(jnp.int32)
    row_second = (got_info[:, 2] * SLOTS + got_info[:, 3]).astype(jnp.int32)

    outgoing = jnp.einsum(
        "zrk,kjc->zjrc",
        spikes.reshape(n_sz, n_sy * SLOTS, -1),
        w_down[0].reshape(-1, n_sy, qw),
        preferred_element_type=jnp.float32,
    ).astype(jnp.bfloat16)
    outgoing = outgoing.reshape(n_sz * n_sy, n_sy * SLOTS, qw)
    back = lax.all_to_all(outgoing, seq_axes, 0, 0, tiled=True)
    table = back.reshape(n_experts, n_sy, SLOTS, qw)
    lanes_e = jnp.arange(n_experts, dtype=jnp.int32)[None, None, :, None]
    lanes_s = jnp.arange(SLOTS, dtype=jnp.int32)[None, None, None, :]

    def pick(row):
        e = (row // SLOTS)[:, :, None, None]
        s = (row % SLOTS)[:, :, None, None]
        return ((e == lanes_e) & (s == lanes_s)).astype(jnp.bfloat16)

    first_out = jnp.einsum(
        "btes,ebsc->btc", pick(row_first), table, preferred_element_type=jnp.float32
    )
    second_out = jnp.einsum(
        "btes,ebsc->btc", pick(row_second), table, preferred_element_type=jnp.float32
    )
    mix_q = (g_first[:, :, None] * first_out + g_second[:, :, None] * second_out).astype(
        jnp.bfloat16
    )

    group_v = mix_q.reshape(n_sy, count, quarter, hd)
    cumulative = jnp.cumsum(group_decay, axis=2)
    scores = jnp.einsum(
        "bthd,bshd->bhts", group_q, group_k, preferred_element_type=jnp.float32
    )
    causal = jnp.arange(count)[:, None] >= jnp.arange(count)[None, :]
    spread = cumulative[:, :, :, None] - cumulative[:, :, None, :]
    decay = jnp.where(causal[None, None], jnp.exp(jnp.minimum(spread, 0.0)), 0.0)
    weights = (scores * decay).astype(jnp.bfloat16)
    intra = jnp.einsum("bhts,bshd->bthd", weights, group_v, preferred_element_type=jnp.float32)

    tail = jnp.exp(cumulative[:, :, -1:] - cumulative)
    scaled_k = group_k.astype(jnp.float32) * jnp.transpose(tail, (0, 2, 1))[:, :, :, None]
    local_states = jnp.einsum(
        "bshd,bshe->bhde", scaled_k, group_v.astype(jnp.float32), precision=highest
    )
    block_total = jnp.exp(cumulative[:, :, -1])

    run = jnp.zeros((quarter, hd, hd), jnp.float32)
    lead = jnp.ones((quarter,), jnp.float32)
    inside, leads = [], []
    for b in range(n_sy):
        inside.append(run)
        leads.append(lead)
        run = block_total[b][:, None, None] * run + local_states[b]
        lead = lead * block_total[b]
    group_state, group_span = run, lead

    growth = jnp.transpose(jnp.exp(cumulative), (0, 2, 1))[:, :, :, None]
    q32 = group_q.astype(jnp.float32)
    near = intra + growth * jnp.einsum(
        "bthd,bhde->bthe", q32, jnp.stack(inside), precision=highest
    )


    def send_home(quarters, total_width):
        assembled = jnp.zeros((count, total_width), jnp.bfloat16)
        for by in range(n_sy):
            piece = lax.dynamic_index_in_dim(quarters, (yi + by) % n_sy, 0, False)
            if by:
                piece = lax.ppermute(piece, "sy", [(i, (i + by) % n_sy) for i in range(n_sy)])
            assembled = lax.dynamic_update_slice(assembled, piece, (0, ((yi - by) % n_sy) * qw))
        return assembled

    expert_mix = send_home(mix_q, width)

    state_rows = quarter * hd

    def pack(value, span):
        span_rows = jnp.zeros((8, hd), jnp.float32).at[0, :quarter].set(span)
        return jnp.concatenate([value.reshape(state_rows, hd), span_rows], axis=0)

    def unpack(packed):
        return packed[:state_rows].reshape(quarter, hd, hd), packed[state_rows, :quarter]

    def shifted(packed, by, first=0):
        pairs = [(i, i + by) for i in range(first, n_sz - by)]
        got_value, got_span = unpack(lax.ppermute(packed, "sz", pairs))
        return got_value, jnp.where(zi >= by, got_span, 1.0)

    def join(earlier, later):
        (v_e, s_e), (v_l, s_l) = earlier, later
        return (s_l[:, None, None] * v_e + v_l, s_e * s_l)

    own = pack(group_state, group_span)
    window = join(shifted(own, 2), shifted(own, 1))
    reach = 2
    while reach < n_sz:
        window = join(shifted(pack(*window), reach, first=1), window)
        reach *= 2
    before = window[0]

    far_scale = growth * jnp.stack(leads)[:, None, :, None]
    total_out = near + far_scale * jnp.einsum("bthd,hde->bthe", q32, before, precision=highest)
    normed = total_out * lax.rsqrt(jnp.mean(total_out * total_out, axis=3, keepdims=True) + 1e-06)
    att_q = normed.astype(jnp.bfloat16).reshape(n_sy, count, qw)
    attended = send_home(att_q, heads * hd)
    return (expert_mix, attended)


def solution(mesh):
    n_dp = mesh.shape["dp"]
    n_seq = mesh.shape["seq"]
    inner = Mesh(mesh.devices.reshape(n_dp, n_seq // GROUP, GROUP), ("dp", "sz", "sy"))
    rows = ("dp", "sz", "sy")
    in_specs = (
        P(rows, None),
        P(rows, None),
        P(),
        P(("sz", "sy"), None, None),
        P(("sz", "sy"), None, None),
        P(("sz", "sy"), None, None),
        P(("sz", "sy"), None),
        P(rows, None),
        P(rows, None),
        P(None, rows),
    )
    out_specs = (P(rows, None), P(rows, None))
    return jax.shard_map(body, mesh=inner, in_specs=in_specs, out_specs=out_specs, check_vma=False)
```
